32 devices in a mesh: seq: 8 (over y, x, core), chan: 4 (over z).
Axes of the slice: x: 2, y: 2, z: 4, core: 2. Of those that a mesh axis runs over, the one named last changes fastest.
Arguments:
- query_proj: bfloat16 [1024, 8192], P('seq', 'chan'), may hold values from -8 to 8
- key_proj: bfloat16 [1024, 8192], P('seq', 'chan'), may hold values from -8 to 8
- value_proj: bfloat16 [1024, 8192], P('seq', 'chan'), may hold values from -6 to 6
- residual: bfloat16 [1024, 8192], P('seq', 'chan'), may hold values from -6 to 6
- out_weight: bfloat16 [8192, 8192], P('chan', 'seq'), may hold values from -0.0625 to 0.0625
Outputs:
- attn_out: bfloat16 [1024, 8192], P('seq', 'chan')
The draws below stay inside these ranges and needn't reach their ends.
All inputs are finite; a program needn't handle non-finite values.
Results may differ from the reference program's by a relative error of at most 0.008.
Values may be sent and summed in bfloat16 or wider, within the bound.
No kernel may reach another device: no remote copies, remote signals or barrier semaphores. Data moves between devices by JAX's collectives and lax.ppermute only.
A program may use at most 64 MiB of HBM per device.

```python
import math
import jax
import jax.numpy as jnp
from jax import lax

D = 8192
HEADS = 64
HEAD_DIM = 128
TOKENS = 1024


def draw_pair(key):
    shape = (TOKENS, HEADS * HEAD_DIM)
    query_key = jax.random.fold_in(key, 11)
    other_key = jax.random.fold_in(key, 12)
    queries = jnp.clip(1.6 * jax.random.normal(query_key, shape, jnp.float32), -8.0, 8.0)
    keys_drawn = jnp.clip(1.6 * jax.random.normal(other_key, shape, jnp.float32), -8.0, 8.0)
    return (queries.astype(jnp.bfloat16), keys_drawn.astype(jnp.bfloat16))


def draw_query_proj(key, part):
    return draw_pair(key)[0]


def draw_key_proj(key, part):
    return draw_pair(key)[1]


def level_of(own_key, dims, shards, low, largest):
    def one(axis_at, parts):
        heights = jax.random.uniform(jax.random.fold_in(jax.random.fold_in(own_key, 6), axis_at), (parts,), jnp.float32, low / len(shards), largest / len(shards))
        return jnp.repeat(jnp.exp(heights), dims[axis_at] // parts).reshape((-1,) + (1,) * (len(dims) - axis_at - 1))

    gain = one(*shards[0])
    for cut in shards[1:]:
        gain = gain * one(*cut)
    return gain


def bell_draw(own_key, shape, width, reach, cuts=(), kind=jnp.bfloat16):
    factor_of = level_of(own_key, shape, cuts, -0.22, 0.18) if cuts else 1.0
    array = jax.random.normal(own_key, shape, jnp.float32) * width * factor_of
    return jnp.minimum(jnp.maximum(array, -reach), reach).astype(kind)


def setup_inputs(seed: int = 0) -> dict:
    splits = jax.random.split(jax.random.key(seed), 6)
    query_proj = draw_query_proj(jax.random.fold_in(splits[5], 71), 0)
    key_proj = draw_key_proj(jax.random.fold_in(splits[5], 71), 0)
    value_proj = bell_draw(splits[2], (TOKENS, D), 1.0, 6.0, ((0, 8), (1, 4)))
    residual = bell_draw(splits[3], (TOKENS, D), 1.0, 6.0, ((0, 8), (1, 4)))
    out_weight = bell_draw(splits[4], (D, D), D ** -0.5, 0.0625, ((0, 4), (1, 8)))
    return dict(query_proj=query_proj, key_proj=key_proj, value_proj=value_proj, residual=residual, out_weight=out_weight)


def attend_head(inputs):
    query_head, key_head, value_head = inputs
    score_scale = 1.0 / math.sqrt(HEAD_DIM)
    scores = jnp.dot(query_head, key_head.T, preferred_element_type=jnp.float32) * score_scale
    positions = jnp.arange(TOKENS, dtype=jnp.int32)
    allowed = positions[None, :] <= positions[:, None]
    scores = jnp.where(allowed, scores, -1e+30)
    row_max = lax.optimization_barrier(jnp.max(scores, axis=-1))
    weights = jnp.where(allowed, jnp.exp(scores - row_max[:, None]), 0.0)
    row_total = lax.optimization_barrier(jnp.sum(weights, axis=-1))
    numer = jnp.dot(weights.astype(jnp.bfloat16), value_head, preferred_element_type=jnp.float32)
    return (numer / row_total[:, None]).astype(jnp.bfloat16)

def reference(query_proj, key_proj, value_proj, residual, out_weight):
    query_heads = query_proj.reshape(TOKENS, HEADS, HEAD_DIM).transpose(1, 0, 2)
    key_heads = key_proj.reshape(TOKENS, HEADS, HEAD_DIM).transpose(1, 0, 2)
    value_heads = value_proj.reshape(TOKENS, HEADS, HEAD_DIM).transpose(1, 0, 2)
    context = lax.map(attend_head, (query_heads, key_heads, value_heads))
    context = context.transpose(1, 0, 2).reshape(TOKENS, D)
    projected = jnp.dot(context, out_weight, preferred_element_type=jnp.float32)
    return (residual.astype(jnp.float32) + projected).astype(jnp.bfloat16)
```

```python
import math

import jax
import jax.numpy as jnp
import numpy as np
from jax import lax
from jax.sharding import Mesh
from jax.sharding import PartitionSpec as P

HEAD_DIM = 128
SEQ = ("hi", "lo")


def cores_per_chip_along_seq(mesh):
    column = mesh.devices[:, 0]
    first = tuple(column[0].coords)
    count = 1
    while count < len(column) and tuple(column[count].coords) == first:
        count += 1
    return count


def gather_seq(x):
    return lax.all_gather(lax.all_gather(x, "hi", axis=0, tiled=True), "lo", axis=0, tiled=True)


def per_device(query_proj, key_proj, value_proj, residual, out_weight):
    seg_rows = query_proj.shape[0]
    feat_width = query_proj.shape[1]
    heads_here = feat_width // HEAD_DIM
    n_hi = lax.axis_size("hi")
    n_lo = lax.axis_size("lo")
    seq_count = n_hi * n_lo
    chan_count = lax.axis_size("chan")
    segment = lax.axis_index("hi") * n_lo + lax.axis_index("lo")
    score_scale = 1.0 / math.sqrt(HEAD_DIM)

    both = gather_seq(jnp.concatenate([key_proj, value_proj], axis=1))
    total_rows = both.shape[0]
    keys = both[:, :feat_width].reshape(total_rows, heads_here, HEAD_DIM)
    values = both[:, feat_width:].reshape(total_rows, heads_here, HEAD_DIM)
    block = np.arange(seq_count)
    block_segment = (block % n_hi) * n_lo + block // n_hi
    key_pos = jnp.asarray(
        (block_segment[:, None] * seg_rows + np.arange(seg_rows)[None, :]).reshape(-1), jnp.int32
    )
    row_pos = segment * seg_rows + jnp.arange(seg_rows, dtype=jnp.int32)
    queries = query_proj.reshape(seg_rows, heads_here, HEAD_DIM)
    scores = (
        jnp.einsum("qhd,khd->hqk", queries, keys, preferred_element_type=jnp.float32) * score_scale
    )
    allowed = (key_pos[None, :] <= row_pos[:, None])[None]
    scores = jnp.where(allowed, scores, -1e30)
    row_max = jnp.max(scores, axis=-1)
    weights = jnp.where(allowed, jnp.exp(scores - row_max[..., None]), 0.0)
    row_total = jnp.sum(weights, axis=-1)
    numer = jnp.einsum(
        "hqk,khd->hqd", weights.astype(jnp.bfloat16), values, preferred_element_type=jnp.float32
    )
    ratio = numer / row_total[..., None]
    local_context = ratio.transpose(1, 0, 2).reshape(seg_rows, feat_width).astype(jnp.bfloat16)

    gathered = gather_seq(local_context)
    sub_rows = seg_rows // chan_count
    grid = gathered.reshape(n_lo, n_hi, chan_count, sub_rows, feat_width)
    block_tokens = seq_count * sub_rows
    rows = grid.transpose(2, 1, 0, 3, 4).reshape(block_tokens * chan_count, feat_width)
    partial_sums = lax.psum_scatter(
        jnp.dot(rows, out_weight, preferred_element_type=jnp.float32).astype(jnp.bfloat16),
        "chan",
        scatter_dimension=0,
        tiled=True,
    ).astype(jnp.float32)
    relaid = lax.all_to_all(
        lax.all_to_all(
            partial_sums.astype(jnp.bfloat16), SEQ, split_axis=0, concat_axis=1, tiled=True
        ),
        "chan",
        split_axis=1,
        concat_axis=0,
        tiled=True,
    ).astype(partial_sums.dtype)
    return (residual.astype(jnp.float32) + relaid).astype(jnp.bfloat16)


def solution(mesh):
    seq_size, chan_size = mesh.devices.shape
    n_lo = cores_per_chip_along_seq(mesh)
    split = Mesh(
        mesh.devices.reshape(seq_size // n_lo, n_lo, chan_size), ("hi", "lo", mesh.axis_names[1])
    )
    rows_cols = P(SEQ, "chan")
    placed = (rows_cols, rows_cols, rows_cols, rows_cols, P("chan", SEQ))
    return jax.shard_map(
        per_device, mesh=split, in_specs=placed, out_specs=rows_cols, check_vma=False
    )
```

```python
import math

import jax
import jax.numpy as jnp
import numpy as np
from jax import lax
from jax.sharding import Mesh
from jax.sharding import PartitionSpec as P

HEAD_DIM = 128
SEQ = ("hi", "lo")


def cores_per_chip_along_seq(mesh):
    column = mesh.devices[:, 0]
    first = tuple(column[0].coords)
    count = 1
    while count < len(column) and tuple(column[count].coords) == first:
        count += 1
    return count


def is_square_of_chips(mesh, n_lo):
    column = mesh.devices[::n_lo, 0]
    if n_lo != 2 or len(column) != 4:
        return False
    coords = [np.array(d.coords) for d in column]
    for i in range(4):
        for flip in (1, 2):
            if np.abs(coords[i] - coords[i ^ flip]).sum() != 1:
                return False
    return True


def swap(axis, flip, n):
    return [(i, i ^ flip) for i in range(n)]


def assemble(pieces, rows, width, dtype):
    out = jnp.zeros((len(pieces) * rows, width), dtype)
    for piece, slot in pieces:
        out = lax.dynamic_update_slice(out, piece, (slot * rows, 0))
    return out


def gather_seq_square(x):
    rows, width = x.shape
    half = rows // 2
    chip = lax.axis_index("hi")
    core = lax.axis_index("lo")
    from_x = lax.ppermute(x, "hi", swap("hi", 1, 4))
    from_y = lax.ppermute(x, "hi", swap("hi", 2, 4))
    diag = jnp.concatenate(
        [
            lax.ppermute(from_y[:half], "hi", swap("hi", 1, 4)),
            lax.ppermute(from_x[half:], "hi", swap("hi", 2, 4)),
        ],
        axis=0,
    )
    mine = [(x, chip), (from_x, chip ^ 1), (from_y, chip ^ 2), (diag, chip ^ 3)]
    pieces = []
    for block, source in mine:
        pieces.append((block, source * 2 + core))
        pieces.append((lax.ppermute(block, "lo", [(0, 1), (1, 0)]), source * 2 + (1 - core)))
    return assemble(pieces, rows, width, x.dtype)


def make_per_device(square):
    def gather_seq(x):
        if square:
            return gather_seq_square(x)
        return lax.all_gather(x, SEQ, axis=0, tiled=True)

    def per_device(query_proj, key_proj, value_proj, residual, out_weight):
        seg_rows = query_proj.shape[0]
        feat_width = query_proj.shape[1]
        heads_here = feat_width // HEAD_DIM
        seq_count = lax.axis_size("hi") * lax.axis_size("lo")
        chan_count = lax.axis_size("chan")
        segment = lax.axis_index("hi") * lax.axis_size("lo") + lax.axis_index("lo")
        score_scale = 1.0 / math.sqrt(HEAD_DIM)

        both = gather_seq(jnp.concatenate([key_proj, value_proj], axis=1))
        total_rows = both.shape[0]
        keys = both[:, :feat_width].reshape(total_rows, heads_here, HEAD_DIM)
        values = both[:, feat_width:].reshape(total_rows, heads_here, HEAD_DIM)
        key_pos = jnp.arange(total_rows, dtype=jnp.int32)
        row_pos = segment * seg_rows + jnp.arange(seg_rows, dtype=jnp.int32)
        queries = query_proj.reshape(seg_rows, heads_here, HEAD_DIM)
        scores = (
            jnp.einsum("qhd,khd->hqk", queries, keys, preferred_element_type=jnp.float32)
            * score_scale
        )
        allowed = (key_pos[None, :] <= row_pos[:, None])[None]
        scores = jnp.where(allowed, scores, -1e30)
        row_max = jnp.max(scores, axis=-1)
        weights = jnp.where(allowed, jnp.exp(scores - row_max[..., None]), 0.0)
        row_total = jnp.sum(weights, axis=-1)
        numer = jnp.einsum(
            "hqk,khd->hqd", weights.astype(jnp.bfloat16), values, preferred_element_type=jnp.float32
        )
        ratio = numer / row_total[..., None]
        local_context = ratio.transpose(1, 0, 2).reshape(seg_rows, feat_width).astype(jnp.bfloat16)

        gathered = gather_seq(local_context)
        sub_rows = seg_rows // chan_count
        grid = gathered.reshape(seq_count, chan_count, sub_rows, feat_width)
        block_tokens = seq_count * sub_rows
        rows = grid.transpose(1, 0, 2, 3).reshape(block_tokens * chan_count, feat_width)
        partial_sums = lax.psum_scatter(
            jnp.dot(rows, out_weight, preferred_element_type=jnp.float32).astype(jnp.bfloat16),
            "chan",
            scatter_dimension=0,
            tiled=True,
        ).astype(jnp.float32)
        relaid = lax.all_to_all(
            lax.all_to_all(
                partial_sums.astype(jnp.bfloat16), SEQ, split_axis=0, concat_axis=1, tiled=True
            ),
            "chan",
            split_axis=1,
            concat_axis=0,
            tiled=True,
        ).astype(partial_sums.dtype)
        return (residual.astype(jnp.float32) + relaid).astype(jnp.bfloat16)

    return per_device


def solution(mesh):
    seq_size, chan_size = mesh.devices.shape
    n_lo = cores_per_chip_along_seq(mesh)
    split = Mesh(
        mesh.devices.reshape(seq_size // n_lo, n_lo, chan_size), ("hi", "lo", mesh.axis_names[1])
    )
    rows_cols = P(SEQ, "chan")
    placed = (rows_cols, rows_cols, rows_cols, rows_cols, P("chan", SEQ))
    return jax.shard_map(
        make_per_device(is_square_of_chips(mesh, n_lo)),
        mesh=split,
        in_specs=placed,
        out_specs=rows_cols,
        check_vma=False,
    )
```

```python
import math

import jax
import jax.numpy as jnp
import numpy as np
from jax import lax
from jax.sharding import Mesh
from jax.sharding import PartitionSpec as P

HEAD_DIM = 128
SEQ = ("hi", "lo")


def cores_per_chip_along_seq(mesh):
    column = mesh.devices[:, 0]
    first = tuple(column[0].coords)
    count = 1
    while count < len(column) and tuple(column[count].coords) == first:
        count += 1
    return count


def is_square_of_chips(mesh, n_lo):
    column = mesh.devices[::n_lo, 0]
    if n_lo != 2 or len(column) != 4:
        return False
    coords = [np.array(d.coords) for d in column]
    for i in range(4):
        for flip in (1, 2):
            if np.abs(coords[i] - coords[i ^ flip]).sum() != 1:
                return False
    return True


def swap(axis, flip, n):
    return [(i, i ^ flip) for i in range(n)]


def gather_seq_square(x):
    half = x.shape[0] // 2
    from_x = lax.ppermute(x, "hi", swap("hi", 1, 4))
    from_y = lax.ppermute(x, "hi", swap("hi", 2, 4))
    diag = jnp.concatenate(
        [
            lax.ppermute(from_y[:half], "hi", swap("hi", 1, 4)),
            lax.ppermute(from_x[half:], "hi", swap("hi", 2, 4)),
        ],
        axis=0,
    )
    pieces = []
    for block in (x, from_x, from_y, diag):
        pieces.append(block)
        pieces.append(lax.ppermute(block, "lo", [(0, 1), (1, 0)]))
    return jnp.concatenate(pieces, axis=0)


def relative_segments(count):
    block = jnp.arange(count, dtype=jnp.int32)
    chip = lax.axis_index("hi") ^ (block // 2)
    core = lax.axis_index("lo") ^ (block % 2)
    return chip * 2 + core


def attention(query_proj, keys_values, segment, key_segment):
    seg_rows, feat_width = query_proj.shape
    heads_here = feat_width // HEAD_DIM
    total_rows = keys_values.shape[0]
    score_scale = 1.0 / math.sqrt(HEAD_DIM)
    keys = keys_values[:, :feat_width].reshape(total_rows, heads_here, HEAD_DIM)
    values = keys_values[:, feat_width:].reshape(total_rows, heads_here, HEAD_DIM)
    key_pos = (
        key_segment[:, None] * seg_rows + jnp.arange(seg_rows, dtype=jnp.int32)[None, :]
    ).reshape(-1)
    row_pos = segment * seg_rows + jnp.arange(seg_rows, dtype=jnp.int32)
    queries = query_proj.reshape(seg_rows, heads_here, HEAD_DIM)
    scores = (
        jnp.einsum("qhd,khd->hqk", queries, keys, preferred_element_type=jnp.float32) * score_scale
    )
    allowed = (key_pos[None, :] <= row_pos[:, None])[None]
    scores = jnp.where(allowed, scores, -1e30)
    row_max = jnp.max(scores, axis=-1)
    weights = jnp.where(allowed, jnp.exp(scores - row_max[..., None]), 0.0)
    row_total = jnp.sum(weights, axis=-1)
    numer = jnp.einsum(
        "hqk,khd->hqd", weights.astype(jnp.bfloat16), values, preferred_element_type=jnp.float32
    )
    ratio = numer / row_total[..., None]
    return ratio.transpose(1, 0, 2).reshape(seg_rows, feat_width).astype(jnp.bfloat16)


def per_device_square(query_proj, key_proj, value_proj, residual, out_weight):
    seg_rows = query_proj.shape[0]
    chips = lax.axis_size("hi")
    chip = lax.axis_index("hi")
    core = lax.axis_index("lo")
    segment = chip * 2 + core
    both = gather_seq_square(jnp.concatenate([key_proj, value_proj], axis=1))
    local_context = attention(query_proj, both, segment, relative_segments(2 * chips))
    rows = gather_seq_square(local_context)
    reduced = lax.psum_scatter(
        jnp.dot(rows, out_weight, preferred_element_type=jnp.float32).astype(jnp.bfloat16),
        "chan",
        scatter_dimension=0,
        tiled=True,
    )
    chans = lax.axis_size("chan")
    received = []
    for t in range(2):
        pairs = []
        for hi in range(chips):
            for lo in range(2):
                for c in range(chans):
                    pairs.append((((hi * 2) + lo) * chans + c, (((hi ^ c) * 2) + (lo ^ t)) * chans + hi))
        received.append(
            lax.ppermute(reduced[t * seg_rows : (t + 1) * seg_rows], ("hi", "lo", "chan"), pairs)
        )
    ordered = jnp.where(
        core == 0,
        jnp.concatenate(received, axis=1),
        jnp.concatenate(received[::-1], axis=1),
    )
    return (residual.astype(jnp.float32) + ordered.astype(jnp.float32)).astype(jnp.bfloat16)


def per_device_general(query_proj, key_proj, value_proj, residual, out_weight):
    seg_rows = query_proj.shape[0]
    feat_width = query_proj.shape[1]
    seq_count = lax.axis_size("hi") * lax.axis_size("lo")
    chan_count = lax.axis_size("chan")
    segment = lax.axis_index("hi") * lax.axis_size("lo") + lax.axis_index("lo")
    both = lax.all_gather(jnp.concatenate([key_proj, value_proj], axis=1), SEQ, axis=0, tiled=True)
    local_context = attention(
        query_proj, both, segment, jnp.arange(seq_count, dtype=jnp.int32)
    )
    gathered = lax.all_gather(local_context, SEQ, axis=0, tiled=True)
    sub_rows = seg_rows // chan_count
    grid = gathered.reshape(seq_count, chan_count, sub_rows, feat_width)
    rows = grid.transpose(1, 0, 2, 3).reshape(seq_count * sub_rows * chan_count, feat_width)
    partial_sums = lax.psum_scatter(
        jnp.dot(rows, out_weight, preferred_element_type=jnp.float32).astype(jnp.bfloat16),
        "chan",
        scatter_dimension=0,
        tiled=True,
    )
    relaid = lax.all_to_all(
        lax.all_to_all(partial_sums, SEQ, split_axis=0, concat_axis=1, tiled=True),
        "chan",
        split_axis=1,
        concat_axis=0,
        tiled=True,
    )
    return (residual.astype(jnp.float32) + relaid.astype(jnp.float32)).astype(jnp.bfloat16)


def solution(mesh):
    seq_size, chan_size = mesh.devices.shape
    n_lo = cores_per_chip_along_seq(mesh)
    split = Mesh(
        mesh.devices.reshape(seq_size // n_lo, n_lo, chan_size), ("hi", "lo", mesh.axis_names[1])
    )
    rows_cols = P(SEQ, "chan")
    placed = (rows_cols, rows_cols, rows_cols, rows_cols, P("chan", SEQ))
    return jax.shard_map(
        per_device_square
        if is_square_of_chips(mesh, n_lo) and chan_size == 4
        else per_device_general,
        mesh=split,
        in_specs=placed,
        out_specs=rows_cols,
        check_vma=False,
    )
```

```python
import math

import jax
import jax.numpy as jnp
import numpy as np
from jax import lax
from jax.sharding import Mesh
from jax.sharding import PartitionSpec as P

HEAD_DIM = 128
SEQ = ("hi", "lo")


def cores_per_chip_along_seq(mesh):
    column = mesh.devices[:, 0]
    first = tuple(column[0].coords)
    count = 1
    while count < len(column) and tuple(column[count].coords) == first:
        count += 1
    return count


def is_square_of_chips(mesh, n_lo):
    column = mesh.devices[::n_lo, 0]
    if n_lo != 2 or len(column) != 4:
        return False
    coords = [np.array(d.coords) for d in column]
    for i in range(4):
        for flip in (1, 2):
            if np.abs(coords[i] - coords[i ^ flip]).sum() != 1:
                return False
    return True


def swap(axis, flip, n):
    return [(i, i ^ flip) for i in range(n)]


def gather_seq_square(x):
    half = x.shape[0] // 2
    from_x = lax.ppermute(x, "hi", swap("hi", 1, 4))
    from_y = lax.ppermute(x, "hi", swap("hi", 2, 4))
    diag = jnp.concatenate(
        [
            lax.ppermute(from_y[:half], "hi", swap("hi", 1, 4)),
            lax.ppermute(from_x[half:], "hi", swap("hi", 2, 4)),
        ],
        axis=0,
    )
    pieces = []
    for block in (x, from_x, from_y, diag):
        pieces.append(block)
        pieces.append(lax.ppermute(block, "lo", [(0, 1), (1, 0)]))
    return pieces


def relative_segment(block):
    return (lax.axis_index("hi") ^ (block // 2)) * 2 + (lax.axis_index("lo") ^ (block % 2))


def attention_blocks(query_proj, key_blocks, value_blocks, segment, key_segments):
    seg_rows, feat_width = query_proj.shape
    heads_here = feat_width // HEAD_DIM
    score_scale = 1.0 / math.sqrt(HEAD_DIM)
    queries = query_proj.reshape(seg_rows, heads_here, HEAD_DIM)
    row_pos = segment * seg_rows + jnp.arange(seg_rows, dtype=jnp.int32)
    scores = []
    masks = []
    for keys, key_segment in zip(key_blocks, key_segments):
        keys = keys.reshape(keys.shape[0], heads_here, HEAD_DIM)
        part = (
            jnp.einsum("qhd,khd->hqk", queries, keys, preferred_element_type=jnp.float32)
            * score_scale
        )
        key_pos = key_segment * seg_rows + jnp.arange(keys.shape[0], dtype=jnp.int32)
        allowed = (key_pos[None, :] <= row_pos[:, None])[None]
        scores.append(jnp.where(allowed, part, -1e30))
        masks.append(allowed)
    row_max = jnp.max(jnp.stack([jnp.max(s, axis=-1) for s in scores]), axis=0)
    row_total = jnp.zeros_like(row_max)
    numer = jnp.zeros((heads_here, seg_rows, HEAD_DIM), jnp.float32)
    for part, allowed, values in zip(scores, masks, value_blocks):
        weights = jnp.where(allowed, jnp.exp(part - row_max[..., None]), 0.0)
        row_total = row_total + jnp.sum(weights, axis=-1)
        values = values.reshape(values.shape[0], heads_here, HEAD_DIM)
        numer = numer + jnp.einsum(
            "hqk,khd->hqd", weights.astype(jnp.bfloat16), values, preferred_element_type=jnp.float32
        )
    ratio = numer / row_total[..., None]
    return ratio.transpose(1, 0, 2).reshape(seg_rows, feat_width).astype(jnp.bfloat16)


def attention(query_proj, keys_values, segment, key_segment):
    feat_width = query_proj.shape[1]
    seg_rows = query_proj.shape[0]
    count = keys_values.shape[0] // seg_rows
    key_blocks = [keys_values[i * seg_rows : (i + 1) * seg_rows, :feat_width] for i in range(count)]
    value_blocks = [keys_values[i * seg_rows : (i + 1) * seg_rows, feat_width:] for i in range(count)]
    return attention_blocks(
        query_proj, key_blocks, value_blocks, segment, [key_segment[i] for i in range(count)]
    )


def per_device_square(query_proj, key_proj, value_proj, residual, out_weight):
    seg_rows = query_proj.shape[0]
    chips = lax.axis_size("hi")
    chans = lax.axis_size("chan")
    chip = lax.axis_index("hi")
    core = lax.axis_index("lo")
    chan = lax.axis_index("chan")
    key_blocks = gather_seq_square(key_proj)
    value_blocks = gather_seq_square(value_proj)
    key_segments = [relative_segment(b) for b in range(len(key_blocks))]
    local_context = attention_blocks(
        query_proj, key_blocks, value_blocks, chip * 2 + core, key_segments
    )
    context_blocks = gather_seq_square(local_context)
    partial = jnp.stack(
        [
            jnp.dot(block, out_weight, preferred_element_type=jnp.float32).astype(jnp.bfloat16)
            for block in context_blocks
        ]
    )
    halves = [None, None]
    for t in range(2):
        for u in range(chans):
            pairs = []
            for hi in range(chips):
                for lo in range(2):
                    for c in range(chans):
                        pairs.append(
                            ((hi * 2 + lo) * chans + c, (((c ^ u) * 2) + (lo ^ t)) * chans + hi)
                        )
            piece = partial[2 * (chip ^ chan ^ u) + t]
            got = lax.ppermute(piece, ("hi", "lo", "chan"), pairs).astype(jnp.float32)
            halves[t] = got if halves[t] is None else halves[t] + got
    ordered = jnp.where(
        core == 0,
        jnp.concatenate(halves, axis=1),
        jnp.concatenate(halves[::-1], axis=1),
    )
    return (residual.astype(jnp.float32) + ordered).astype(jnp.bfloat16)


def per_device_general(query_proj, key_proj, value_proj, residual, out_weight):
    seg_rows = query_proj.shape[0]
    feat_width = query_proj.shape[1]
    seq_count = lax.axis_size("hi") * lax.axis_size("lo")
    chan_count = lax.axis_size("chan")
    segment = lax.axis_index("hi") * lax.axis_size("lo") + lax.axis_index("lo")
    both = lax.all_gather(jnp.concatenate([key_proj, value_proj], axis=1), SEQ, axis=0, tiled=True)
    local_context = attention(
        query_proj, both, segment, jnp.arange(seq_count, dtype=jnp.int32)
    )
    gathered = lax.all_gather(local_context, SEQ, axis=0, tiled=True)
    sub_rows = seg_rows // chan_count
    grid = gathered.reshape(seq_count, chan_count, sub_rows, feat_width)
    rows = grid.transpose(1, 0, 2, 3).reshape(seq_count * sub_rows * chan_count, feat_width)
    partial_sums = lax.psum_scatter(
        jnp.dot(rows, out_weight, preferred_element_type=jnp.float32).astype(jnp.bfloat16),
        "chan",
        scatter_dimension=0,
        tiled=True,
    )
    relaid = lax.all_to_all(
        lax.all_to_all(partial_sums, SEQ, split_axis=0, concat_axis=1, tiled=True),
        "chan",
        split_axis=1,
        concat_axis=0,
        tiled=True,
    )
    return (residual.astype(jnp.float32) + relaid.astype(jnp.float32)).astype(jnp.bfloat16)


def solution(mesh):
    seq_size, chan_size = mesh.devices.shape
    n_lo = cores_per_chip_along_seq(mesh)
    split = Mesh(
        mesh.devices.reshape(seq_size // n_lo, n_lo, chan_size), ("hi", "lo", mesh.axis_names[1])
    )
    rows_cols = P(SEQ, "chan")
    placed = (rows_cols, rows_cols, rows_cols, rows_cols, P("chan", SEQ))
    return jax.shard_map(
        per_device_square
        if is_square_of_chips(mesh, n_lo) and chan_size == 4
        else per_device_general,
        mesh=split,
        in_specs=placed,
        out_specs=rows_cols,
        check_vma=False,
    )
```

```python
import math

import jax
import jax.numpy as jnp
import numpy as np
from jax import lax
from jax.sharding import Mesh
from jax.sharding import PartitionSpec as P

HEAD_DIM = 128
SEQ = ("hi", "lo")


def cores_per_chip_along_seq(mesh):
    column = mesh.devices[:, 0]
    first = tuple(column[0].coords)
    count = 1
    while count < len(column) and tuple(column[count].coords) == first:
        count += 1
    return count


def is_square_of_chips(mesh, n_lo):
    column = mesh.devices[::n_lo, 0]
    if n_lo != 2 or len(column) != 4:
        return False
    coords = [np.array(d.coords) for d in column]
    for i in range(4):
        for flip in (1, 2):
            if np.abs(coords[i] - coords[i ^ flip]).sum() != 1:
                return False
    return True


def swap(axis, flip, n):
    return [(i, i ^ flip) for i in range(n)]


def assemble(pieces, rows, width, dtype):
    out = jnp.zeros((len(pieces) * rows, width), dtype)
    for piece, slot in pieces:
        out = lax.dynamic_update_slice(out, piece, (slot * rows, 0))
    return out


def gather_seq_square(x):
    rows, width = x.shape
    half = rows // 2
    chip = lax.axis_index("hi")
    core = lax.axis_index("lo")
    from_x = lax.ppermute(x, "hi", swap("hi", 1, 4))
    from_y = lax.ppermute(x, "hi", swap("hi", 2, 4))
    diag = jnp.concatenate(
        [
            lax.ppermute(from_y[:half], "hi", swap("hi", 1, 4)),
            lax.ppermute(from_x[half:], "hi", swap("hi", 2, 4)),
        ],
        axis=0,
    )
    mine = [(x, chip), (from_x, chip ^ 1), (from_y, chip ^ 2), (diag, chip ^ 3)]
    pieces = []
    for block, source in mine:
        pieces.append((block, source * 2 + core))
        pieces.append((lax.ppermute(block, "lo", [(0, 1), (1, 0)]), source * 2 + (1 - core)))
    return assemble(pieces, rows, width, x.dtype)


def make_per_device(square):
    def gather_seq(x):
        if square:
            return gather_seq_square(x)
        return lax.all_gather(x, SEQ, axis=0, tiled=True)

    def per_device(query_proj, key_proj, value_proj, residual, out_weight):
        seg_rows = query_proj.shape[0]
        feat_width = query_proj.shape[1]
        heads_here = feat_width // HEAD_DIM
        seq_count = lax.axis_size("hi") * lax.axis_size("lo")
        chan_count = lax.axis_size("chan")
        segment = lax.axis_index("hi") * lax.axis_size("lo") + lax.axis_index("lo")
        score_scale = 1.0 / math.sqrt(HEAD_DIM)

        both = gather_seq(jnp.concatenate([key_proj, value_proj], axis=1))
        total_rows = both.shape[0]
        keys = both[:, :feat_width].reshape(total_rows, heads_here, HEAD_DIM)
        values = both[:, feat_width:].reshape(total_rows, heads_here, HEAD_DIM)
        key_pos = jnp.arange(total_rows, dtype=jnp.int32)
        row_pos = segment * seg_rows + jnp.arange(seg_rows, dtype=jnp.int32)
        queries = query_proj.reshape(seg_rows, heads_here, HEAD_DIM)
        scores = (
            jnp.einsum("qhd,khd->hqk", queries, keys, preferred_element_type=jnp.float32)
            * score_scale
        )
        allowed = (key_pos[None, :] <= row_pos[:, None])[None]
        scores = jnp.where(allowed, scores, -1e30)
        row_max = jnp.max(scores, axis=-1)
        weights = jnp.where(allowed, jnp.exp(scores - row_max[..., None]), 0.0)
        row_total = jnp.sum(weights, axis=-1)
        numer = jnp.einsum(
            "hqk,khd->hqd", weights.astype(jnp.bfloat16), values, preferred_element_type=jnp.float32
        )
        ratio = numer / row_total[..., None]
        local_context = ratio.transpose(1, 0, 2).reshape(seg_rows, feat_width).astype(jnp.bfloat16)

        gathered = gather_seq(local_context)
        group = seq_count // chan_count
        chunks = 2
        width = out_weight.shape[1] // chunks
        reduced = []
        for j in range(chunks):
            partial = jnp.dot(
                gathered, out_weight[:, j * width : (j + 1) * width], preferred_element_type=jnp.float32
            ).astype(jnp.bfloat16)
            by_row = lax.all_to_all(partial, SEQ, split_axis=0, concat_axis=1, tiled=True)
            reduced.append(
                lax.psum_scatter(by_row, "chan", scatter_dimension=1, tiled=True)
            )
        ordered = jnp.concatenate(
            [part[:, b * width : (b + 1) * width] for b in range(group) for part in reduced], axis=1
        )
        return (residual.astype(jnp.float32) + ordered.astype(jnp.float32)).astype(jnp.bfloat16)

    return per_device


def solution(mesh):
    seq_size, chan_size = mesh.devices.shape
    n_lo = cores_per_chip_along_seq(mesh)
    split = Mesh(
        mesh.devices.reshape(seq_size // n_lo, n_lo, chan_size), ("hi", "lo", mesh.axis_names[1])
    )
    rows_cols = P(SEQ, "chan")
    placed = (rows_cols, rows_cols, rows_cols, rows_cols, P("chan", SEQ))
    return jax.shard_map(
        make_per_device(is_square_of_chips(mesh, n_lo)),
        mesh=split,
        in_specs=placed,
        out_specs=rows_cols,
        check_vma=False,
    )
```

```python
import math

import jax
import jax.numpy as jnp
import numpy as np
from jax import lax
from jax.sharding import Mesh
from jax.sharding import PartitionSpec as P

HEAD_DIM = 128
SEQ = ("hi", "lo")


def cores_per_chip_along_seq(mesh):
    column = mesh.devices[:, 0]
    first = tuple(column[0].coords)
    count = 1
    while count < len(column) and tuple(column[count].coords) == first:
        count += 1
    return count


def is_square_of_chips(mesh, n_lo):
    column = mesh.devices[::n_lo, 0]
    if n_lo != 2 or len(column) != 4:
        return False
    coords = [np.array(d.coords) for d in column]
    for i in range(4):
        for flip in (1, 2):
            if np.abs(coords[i] - coords[i ^ flip]).sum() != 1:
                return False
    return True


def swap(axis, flip, n):
    return [(i, i ^ flip) for i in range(n)]


def assemble(pieces, rows, width, dtype):
    out = jnp.zeros((len(pieces) * rows, width), dtype)
    for piece, slot in pieces:
        out = lax.dynamic_update_slice(out, piece, (slot * rows, 0))
    return out


def gather_seq_square(x):
    rows, width = x.shape
    half = rows // 2
    chip = lax.axis_index("hi")
    core = lax.axis_index("lo")
    from_x = lax.ppermute(x, "hi", swap("hi", 1, 4))
    from_y = lax.ppermute(x, "hi", swap("hi", 2, 4))
    diag = jnp.concatenate(
        [
            lax.ppermute(from_y[:half], "hi", swap("hi", 1, 4)),
            lax.ppermute(from_x[half:], "hi", swap("hi", 2, 4)),
        ],
        axis=0,
    )
    mine = [(x, chip), (from_x, chip ^ 1), (from_y, chip ^ 2), (diag, chip ^ 3)]
    pieces = []
    for block, source in mine:
        pieces.append((block, source * 2 + core))
        pieces.append((lax.ppermute(block, "lo", [(0, 1), (1, 0)]), source * 2 + (1 - core)))
    return assemble(pieces, rows, width, x.dtype)


def a2a_seq_square(x):
    rows = x.shape[0] // 8
    width = x.shape[1]
    chip = lax.axis_index("hi")
    core = lax.axis_index("lo")
    own = chip * 2 + core
    out = jnp.zeros((rows, 8 * width), x.dtype)
    out = lax.dynamic_update_slice(out, lax.dynamic_slice_in_dim(x, own * rows, rows, 0), (0, own * width))
    for r in range(4):
        for t in range(2):
            if r == 0 and t == 0:
                continue
            other = (chip ^ r) * 2 + (core ^ t)
            pairs = [(h * 2 + l, (h ^ r) * 2 + (l ^ t)) for h in range(4) for l in range(2)]
            got = lax.ppermute(lax.dynamic_slice_in_dim(x, other * rows, rows, 0), SEQ, pairs)
            out = lax.dynamic_update_slice(out, got, (0, other * width))
    return out


def make_per_device(square):
    def gather_seq(x):
        if square:
            return gather_seq_square(x)
        return lax.all_gather(x, SEQ, axis=0, tiled=True)

    def per_device(query_proj, key_proj, value_proj, residual, out_weight):
        seg_rows = query_proj.shape[0]
        feat_width = query_proj.shape[1]
        heads_here = feat_width // HEAD_DIM
        seq_count = lax.axis_size("hi") * lax.axis_size("lo")
        chan_count = lax.axis_size("chan")
        segment = lax.axis_index("hi") * lax.axis_size("lo") + lax.axis_index("lo")
        score_scale = 1.0 / math.sqrt(HEAD_DIM)

        both = gather_seq(jnp.concatenate([key_proj, value_proj], axis=1))
        total_rows = both.shape[0]
        keys = both[:, :feat_width].reshape(total_rows, heads_here, HEAD_DIM)
        values = both[:, feat_width:].reshape(total_rows, heads_here, HEAD_DIM)
        key_pos = jnp.arange(total_rows, dtype=jnp.int32)
        row_pos = segment * seg_rows + jnp.arange(seg_rows, dtype=jnp.int32)
        queries = query_proj.reshape(seg_rows, heads_here, HEAD_DIM)
        scores = (
            jnp.einsum("qhd,khd->hqk", queries, keys, preferred_element_type=jnp.float32)
            * score_scale
        )
        allowed = (key_pos[None, :] <= row_pos[:, None])[None]
        scores = jnp.where(allowed, scores, -1e30)
        row_max = jnp.max(scores, axis=-1)
        weights = jnp.where(allowed, jnp.exp(scores - row_max[..., None]), 0.0)
        row_total = jnp.sum(weights, axis=-1)
        numer = jnp.einsum(
            "hqk,khd->hqd", weights.astype(jnp.bfloat16), values, preferred_element_type=jnp.float32
        )
        ratio = numer / row_total[..., None]
        local_context = ratio.transpose(1, 0, 2).reshape(seg_rows, feat_width).astype(jnp.bfloat16)

        gathered = gather_seq(local_context)
        group = seq_count // chan_count
        chunks = 2
        width = out_weight.shape[1] // chunks
        reduced = []
        for j in range(chunks):
            partial = jnp.dot(
                gathered, out_weight[:, j * width : (j + 1) * width], preferred_element_type=jnp.float32
            ).astype(jnp.bfloat16)
            if square:
                by_row = a2a_seq_square(partial)
            else:
                by_row = lax.all_to_all(partial, SEQ, split_axis=0, concat_axis=1, tiled=True)
            reduced.append(
                lax.psum_scatter(by_row, "chan", scatter_dimension=1, tiled=True)
            )
        ordered = jnp.concatenate(
            [part[:, b * width : (b + 1) * width] for b in range(group) for part in reduced], axis=1
        )
        return (residual.astype(jnp.float32) + ordered.astype(jnp.float32)).astype(jnp.bfloat16)

    return per_device


def solution(mesh):
    seq_size, chan_size = mesh.devices.shape
    n_lo = cores_per_chip_along_seq(mesh)
    split = Mesh(
        mesh.devices.reshape(seq_size // n_lo, n_lo, chan_size), ("hi", "lo", mesh.axis_names[1])
    )
    rows_cols = P(SEQ, "chan")
    placed = (rows_cols, rows_cols, rows_cols, rows_cols, P("chan", SEQ))
    return jax.shard_map(
        make_per_device(is_square_of_chips(mesh, n_lo)),
        mesh=split,
        in_specs=placed,
        out_specs=rows_cols,
        check_vma=False,
    )
```

```python
import math

import jax
import jax.numpy as jnp
import numpy as np
from jax import lax
from jax.sharding import Mesh
from jax.sharding import PartitionSpec as P

HEAD_DIM = 128
SEQ = ("hi", "lo")


def cores_per_chip_along_seq(mesh):
    column = mesh.devices[:, 0]
    first = tuple(column[0].coords)
    count = 1
    while count < len(column) and tuple(column[count].coords) == first:
        count += 1
    return count


def is_square_of_chips(mesh, n_lo):
    column = mesh.devices[::n_lo, 0]
    if n_lo != 2 or len(column) != 4:
        return False
    coords = [np.array(d.coords) for d in column]
    for i in range(4):
        for flip in (1, 2):
            if np.abs(coords[i] - coords[i ^ flip]).sum() != 1:
                return False
    return True


def swap(axis, flip, n):
    return [(i, i ^ flip) for i in range(n)]


def assemble(pieces, rows, width, dtype):
    out = jnp.zeros((len(pieces) * rows, width), dtype)
    for piece, slot in pieces:
        out = lax.dynamic_update_slice(out, piece, (slot * rows, 0))
    return out


def gather_seq_square(x):
    rows, width = x.shape
    half = rows // 2
    chip = lax.axis_index("hi")
    core = lax.axis_index("lo")
    from_x = lax.ppermute(x, "hi", swap("hi", 1, 4))
    from_y = lax.ppermute(x, "hi", swap("hi", 2, 4))
    diag = jnp.concatenate(
        [
            lax.ppermute(from_y[:half], "hi", swap("hi", 1, 4)),
            lax.ppermute(from_x[half:], "hi", swap("hi", 2, 4)),
        ],
        axis=0,
    )
    mine = [(x, chip), (from_x, chip ^ 1), (from_y, chip ^ 2), (diag, chip ^ 3)]
    pieces = []
    for block, source in mine:
        pieces.append((block, source * 2 + core))
        pieces.append((lax.ppermute(block, "lo", [(0, 1), (1, 0)]), source * 2 + (1 - core)))
    return assemble(pieces, rows, width, x.dtype)


def gather_blocks_square(x):
    half = x.shape[0] // 2
    from_x = lax.ppermute(x, "hi", swap("hi", 1, 4))
    from_y = lax.ppermute(x, "hi", swap("hi", 2, 4))
    diag = jnp.concatenate(
        [
            lax.ppermute(from_y[:half], "hi", swap("hi", 1, 4)),
            lax.ppermute(from_x[half:], "hi", swap("hi", 2, 4)),
        ],
        axis=0,
    )
    blocks = []
    for block in (x, from_x, from_y, diag):
        blocks.append(block)
        blocks.append(lax.ppermute(block, "lo", [(0, 1), (1, 0)]))
    return blocks


def attention_by_head(queries, key_blocks, value_blocks, row_pos, key_starts):
    score_scale = 1.0 / math.sqrt(HEAD_DIM)
    scores = []
    masks = []
    for keys, start in zip(key_blocks, key_starts):
        part = (
            jnp.einsum("hqd,hkd->hqk", queries, keys, preferred_element_type=jnp.float32)
            * score_scale
        )
        key_pos = start + jnp.arange(keys.shape[1], dtype=jnp.int32)
        allowed = (key_pos[None, :] <= row_pos[:, None])[None]
        scores.append(jnp.where(allowed, part, -1e30))
        masks.append(allowed)
    row_max = scores[0].max(axis=-1)
    for part in scores[1:]:
        row_max = jnp.maximum(row_max, part.max(axis=-1))
    row_total = None
    numer = None
    for part, allowed, values in zip(scores, masks, value_blocks):
        weights = jnp.where(allowed, jnp.exp(part - row_max[..., None]), 0.0)
        total = jnp.sum(weights, axis=-1)
        term = jnp.einsum(
            "hqk,hkd->hqd", weights.astype(jnp.bfloat16), values, preferred_element_type=jnp.float32
        )
        row_total = total if row_total is None else row_total + total
        numer = term if numer is None else numer + term
    return numer / row_total[..., None]


def make_per_device(square):
    def gather_seq(x):
        if square:
            return gather_seq_square(x)
        return lax.all_gather(x, SEQ, axis=0, tiled=True)

    def per_device(query_proj, key_proj, value_proj, residual, out_weight):
        seg_rows = query_proj.shape[0]
        feat_width = query_proj.shape[1]
        heads_here = feat_width // HEAD_DIM
        seq_count = lax.axis_size("hi") * lax.axis_size("lo")
        chan_count = lax.axis_size("chan")
        segment = lax.axis_index("hi") * lax.axis_size("lo") + lax.axis_index("lo")
        score_scale = 1.0 / math.sqrt(HEAD_DIM)

        row_pos = segment * seg_rows + jnp.arange(seg_rows, dtype=jnp.int32)
        if square:
            def by_head(x):
                return x.reshape(seg_rows, heads_here, HEAD_DIM).transpose(1, 0, 2)

            key_blocks = gather_blocks_square(by_head(key_proj))
            value_blocks = gather_blocks_square(by_head(value_proj))
            chip = lax.axis_index("hi")
            core = lax.axis_index("lo")
            key_starts = [
                ((chip ^ (b // 2)) * 2 + (core ^ (b % 2))) * seg_rows for b in range(len(key_blocks))
            ]
            ratio = attention_by_head(by_head(query_proj), key_blocks, value_blocks, row_pos, key_starts)
        else:
            both = gather_seq(jnp.concatenate([key_proj, value_proj], axis=1))
            total_rows = both.shape[0]
            keys = both[:, :feat_width].reshape(total_rows, heads_here, HEAD_DIM)
            values = both[:, feat_width:].reshape(total_rows, heads_here, HEAD_DIM)
            key_pos = jnp.arange(total_rows, dtype=jnp.int32)
            queries = query_proj.reshape(seg_rows, heads_here, HEAD_DIM)
            scores = (
                jnp.einsum("qhd,khd->hqk", queries, keys, preferred_element_type=jnp.float32)
                * score_scale
            )
            allowed = (key_pos[None, :] <= row_pos[:, None])[None]
            scores = jnp.where(allowed, scores, -1e30)
            row_max = jnp.max(scores, axis=-1)
            weights = jnp.where(allowed, jnp.exp(scores - row_max[..., None]), 0.0)
            row_total = jnp.sum(weights, axis=-1)
            numer = jnp.einsum(
                "hqk,khd->hqd", weights.astype(jnp.bfloat16), values, preferred_element_type=jnp.float32
            )
            ratio = numer / row_total[..., None]
        local_context = ratio.transpose(1, 0, 2).reshape(seg_rows, feat_width).astype(jnp.bfloat16)

        gathered = gather_seq(local_context)
        group = seq_count // chan_count
        chunks = 2
        width = out_weight.shape[1] // chunks
        reduced = []
        for j in range(chunks):
            partial = jnp.dot(
                gathered, out_weight[:, j * width : (j + 1) * width], preferred_element_type=jnp.float32
            ).astype(jnp.bfloat16)
            by_row = lax.all_to_all(partial, SEQ, split_axis=0, concat_axis=1, tiled=True)
            reduced.append(
                lax.psum_scatter(by_row, "chan", scatter_dimension=1, tiled=True)
            )
        ordered = jnp.concatenate(
            [part[:, b * width : (b + 1) * width] for b in range(group) for part in reduced], axis=1
        )
        return (residual.astype(jnp.float32) + ordered.astype(jnp.float32)).astype(jnp.bfloat16)

    return per_device


def solution(mesh):
    seq_size, chan_size = mesh.devices.shape
    n_lo = cores_per_chip_along_seq(mesh)
    split = Mesh(
        mesh.devices.reshape(seq_size // n_lo, n_lo, chan_size), ("hi", "lo", mesh.axis_names[1])
    )
    rows_cols = P(SEQ, "chan")
    placed = (rows_cols, rows_cols, rows_cols, rows_cols, P("chan", SEQ))
    return jax.shard_map(
        make_per_device(is_square_of_chips(mesh, n_lo)),
        mesh=split,
        in_specs=placed,
        out_specs=rows_cols,
        check_vma=False,
    )
```

```python
import math

import jax
import jax.numpy as jnp
import numpy as np
from jax import lax
from jax.sharding import Mesh
from jax.sharding import PartitionSpec as P

HEAD_DIM = 128
SEQ = ("hi", "lo")


def cores_per_chip_along_seq(mesh):
    column = mesh.devices[:, 0]
    first = tuple(column[0].coords)
    count = 1
    while count < len(column) and tuple(column[count].coords) == first:
        count += 1
    return count


def is_square_of_chips(mesh, n_lo):
    column = mesh.devices[::n_lo, 0]
    if n_lo != 2 or len(column) != 4:
        return False
    coords = [np.array(d.coords) for d in column]
    for i in range(4):
        for flip in (1, 2):
            if np.abs(coords[i] - coords[i ^ flip]).sum() != 1:
                return False
    return True


def swap(axis, flip, n):
    return [(i, i ^ flip) for i in range(n)]


def assemble(pieces, rows, width, dtype):
    out = jnp.zeros((len(pieces) * rows, width), dtype)
    for piece, slot in pieces:
        out = lax.dynamic_update_slice(out, piece, (slot * rows, 0))
    return out


def gather_seq_square(x):
    rows, width = x.shape
    half = rows // 2
    chip = lax.axis_index("hi")
    core = lax.axis_index("lo")
    from_x = lax.ppermute(x, "hi", swap("hi", 1, 4))
    from_y = lax.ppermute(x, "hi", swap("hi", 2, 4))
    diag = jnp.concatenate(
        [
            lax.ppermute(from_y[:half], "hi", swap("hi", 1, 4)),
            lax.ppermute(from_x[half:], "hi", swap("hi", 2, 4)),
        ],
        axis=0,
    )
    mine = [(x, chip), (from_x, chip ^ 1), (from_y, chip ^ 2), (diag, chip ^ 3)]
    pieces = []
    for block, source in mine:
        pieces.append((block, source * 2 + core))
        pieces.append((lax.ppermute(block, "lo", [(0, 1), (1, 0)]), source * 2 + (1 - core)))
    return assemble(pieces, rows, width, x.dtype)


def gather_blocks_square(x):
    half = x.shape[0] // 2
    from_x = lax.ppermute(x, "hi", swap("hi", 1, 4))
    from_y = lax.ppermute(x, "hi", swap("hi", 2, 4))
    diag = jnp.concatenate(
        [
            lax.ppermute(from_y[:half], "hi", swap("hi", 1, 4)),
            lax.ppermute(from_x[half:], "hi", swap("hi", 2, 4)),
        ],
        axis=0,
    )
    blocks = []
    for block in (x, from_x, from_y, diag):
        blocks.append(block)
        blocks.append(lax.ppermute(block, "lo", [(0, 1), (1, 0)]))
    return blocks


def attention_by_head(queries, key_blocks, value_blocks, row_pos, key_starts):
    score_scale = 1.0 / math.sqrt(HEAD_DIM)
    scores = []
    masks = []
    for keys, start in zip(key_blocks, key_starts):
        part = (
            jnp.einsum("hqd,hkd->hqk", queries, keys, preferred_element_type=jnp.float32)
            * score_scale
        )
        key_pos = start + jnp.arange(keys.shape[1], dtype=jnp.int32)
        allowed = (key_pos[None, :] <= row_pos[:, None])[None]
        scores.append(jnp.where(allowed, part, -1e30))
        masks.append(allowed)
    row_max = scores[0].max(axis=-1)
    for part in scores[1:]:
        row_max = jnp.maximum(row_max, part.max(axis=-1))
    row_total = None
    numer = None
    for part, allowed, values in zip(scores, masks, value_blocks):
        weights = jnp.where(allowed, jnp.exp(part - row_max[..., None]), 0.0)
        total = jnp.sum(weights, axis=-1)
        term = jnp.einsum(
            "hqk,hkd->hqd", weights.astype(jnp.bfloat16), values, preferred_element_type=jnp.float32
        )
        row_total = total if row_total is None else row_total + total
        numer = term if numer is None else numer + term
    return numer / row_total[..., None]


def make_per_device(square):
    def gather_seq(x):
        if square:
            return gather_seq_square(x)
        return lax.all_gather(x, SEQ, axis=0, tiled=True)

    def per_device(query_proj, key_proj, value_proj, residual, out_weight):
        seg_rows = query_proj.shape[0]
        feat_width = query_proj.shape[1]
        heads_here = feat_width // HEAD_DIM
        seq_count = lax.axis_size("hi") * lax.axis_size("lo")
        chan_count = lax.axis_size("chan")
        segment = lax.axis_index("hi") * lax.axis_size("lo") + lax.axis_index("lo")
        score_scale = 1.0 / math.sqrt(HEAD_DIM)

        row_pos = segment * seg_rows + jnp.arange(seg_rows, dtype=jnp.int32)
        if square:
            def by_head(x):
                return x.reshape(seg_rows, heads_here, HEAD_DIM).transpose(1, 0, 2)

            key_blocks = gather_blocks_square(by_head(key_proj))
            value_blocks = gather_blocks_square(by_head(value_proj))
            chip = lax.axis_index("hi")
            core = lax.axis_index("lo")
            key_starts = [
                ((chip ^ (b // 2)) * 2 + (core ^ (b % 2))) * seg_rows for b in range(len(key_blocks))
            ]
            ratio = attention_by_head(by_head(query_proj), key_blocks, value_blocks, row_pos, key_starts)
        else:
            both = gather_seq(jnp.concatenate([key_proj, value_proj], axis=1))
            total_rows = both.shape[0]
            keys = both[:, :feat_width].reshape(total_rows, heads_here, HEAD_DIM)
            values = both[:, feat_width:].reshape(total_rows, heads_here, HEAD_DIM)
            key_pos = jnp.arange(total_rows, dtype=jnp.int32)
            queries = query_proj.reshape(seg_rows, heads_here, HEAD_DIM)
            scores = (
                jnp.einsum("qhd,khd->hqk", queries, keys, preferred_element_type=jnp.float32)
                * score_scale
            )
            allowed = (key_pos[None, :] <= row_pos[:, None])[None]
            scores = jnp.where(allowed, scores, -1e30)
            row_max = jnp.max(scores, axis=-1)
            weights = jnp.where(allowed, jnp.exp(scores - row_max[..., None]), 0.0)
            row_total = jnp.sum(weights, axis=-1)
            numer = jnp.einsum(
                "hqk,khd->hqd", weights.astype(jnp.bfloat16), values, preferred_element_type=jnp.float32
            )
            ratio = numer / row_total[..., None]
        local_context = ratio.transpose(1, 0, 2).reshape(seg_rows, feat_width).astype(jnp.bfloat16)

        gathered = gather_seq(local_context)
        group = seq_count // chan_count
        total = out_weight.shape[1]
        widths = [total // 4, total - total // 4]
        reduced = []
        offset = 0
        for width in widths:
            partial = jnp.dot(
                gathered, out_weight[:, offset : offset + width], preferred_element_type=jnp.float32
            ).astype(jnp.bfloat16)
            offset += width
            by_row = lax.all_to_all(partial, SEQ, split_axis=0, concat_axis=1, tiled=True)
            reduced.append(
                lax.psum_scatter(by_row, "chan", scatter_dimension=1, tiled=True)
            )
        ordered = jnp.concatenate(
            [
                part[:, b * width : (b + 1) * width]
                for b in range(group)
                for part, width in zip(reduced, widths)
            ],
            axis=1,
        )
        return (residual.astype(jnp.float32) + ordered.astype(jnp.float32)).astype(jnp.bfloat16)

    return per_device


def solution(mesh):
    seq_size, chan_size = mesh.devices.shape
    n_lo = cores_per_chip_along_seq(mesh)
    split = Mesh(
        mesh.devices.reshape(seq_size // n_lo, n_lo, chan_size), ("hi", "lo", mesh.axis_names[1])
    )
    rows_cols = P(SEQ, "chan")
    placed = (rows_cols, rows_cols, rows_cols, rows_cols, P("chan", SEQ))
    return jax.shard_map(
        make_per_device(is_square_of_chips(mesh, n_lo)),
        mesh=split,
        in_specs=placed,
        out_specs=rows_cols,
        check_vma=False,
    )
```

```python
import math

import jax
import jax.numpy as jnp
import numpy as np
from jax import lax
from jax.sharding import Mesh
from jax.sharding import PartitionSpec as P

HEAD_DIM = 128
SEQ = ("hi", "lo")


def cores_per_chip_along_seq(mesh):
    column = mesh.devices[:, 0]
    first = tuple(column[0].coords)
    count = 1
    while count < len(column) and tuple(column[count].coords) == first:
        count += 1
    return count


def is_square_of_chips(mesh, n_lo):
    column = mesh.devices[::n_lo, 0]
    if n_lo != 2 or len(column) != 4:
        return False
    coords = [np.array(d.coords) for d in column]
    for i in range(4):
        for flip in (1, 2):
            if np.abs(coords[i] - coords[i ^ flip]).sum() != 1:
                return False
    return True


def swap(axis, flip, n):
    return [(i, i ^ flip) for i in range(n)]


def assemble(pieces, rows, width, dtype):
    out = jnp.zeros((len(pieces) * rows, width), dtype)
    for piece, slot in pieces:
        out = lax.dynamic_update_slice(out, piece, (slot * rows, 0))
    return out


def gather_seq_square(x):
    rows, width = x.shape
    half = rows // 2
    chip = lax.axis_index("hi")
    core = lax.axis_index("lo")
    from_x = lax.ppermute(x, "hi", swap("hi", 1, 4))
    from_y = lax.ppermute(x, "hi", swap("hi", 2, 4))
    diag = jnp.concatenate(
        [
            lax.ppermute(from_y[:half], "hi", swap("hi", 1, 4)),
            lax.ppermute(from_x[half:], "hi", swap("hi", 2, 4)),
        ],
        axis=0,
    )
    mine = [(x, chip), (from_x, chip ^ 1), (from_y, chip ^ 2), (diag, chip ^ 3)]
    pieces = []
    for block, source in mine:
        pieces.append((block, source * 2 + core))
        pieces.append((lax.ppermute(block, "lo", [(0, 1), (1, 0)]), source * 2 + (1 - core)))
    return assemble(pieces, rows, width, x.dtype)


def gather_blocks_square(x):
    half = x.shape[0] // 2
    from_x = lax.ppermute(x, "hi", swap("hi", 1, 4))
    from_y = lax.ppermute(x, "hi", swap("hi", 2, 4))
    diag = jnp.concatenate(
        [
            lax.ppermute(from_y[:half], "hi", swap("hi", 1, 4)),
            lax.ppermute(from_x[half:], "hi", swap("hi", 2, 4)),
        ],
        axis=0,
    )
    blocks = []
    for block in (x, from_x, from_y, diag):
        blocks.append(block)
        blocks.append(lax.ppermute(block, "lo", [(0, 1), (1, 0)]))
    return blocks


def attention_by_head(queries, key_blocks, value_blocks, row_pos, key_starts):
    score_scale = 1.0 / math.sqrt(HEAD_DIM)
    scores = []
    masks = []
    for keys, start in zip(key_blocks, key_starts):
        part = (
            jnp.einsum("hqd,hkd->hqk", queries, keys, preferred_element_type=jnp.float32)
            * score_scale
        )
        key_pos = start + jnp.arange(keys.shape[1], dtype=jnp.int32)
        allowed = (key_pos[None, :] <= row_pos[:, None])[None]
        scores.append(jnp.where(allowed, part, -1e30))
        masks.append(allowed)
    row_max = scores[0].max(axis=-1)
    for part in scores[1:]:
        row_max = jnp.maximum(row_max, part.max(axis=-1))
    row_total = None
    numer = None
    for part, allowed, values in zip(scores, masks, value_blocks):
        weights = jnp.where(allowed, jnp.exp(part - row_max[..., None]), 0.0)
        total = jnp.sum(weights, axis=-1)
        term = jnp.einsum(
            "hqk,hkd->hqd", weights.astype(jnp.bfloat16), values, preferred_element_type=jnp.float32
        )
        row_total = total if row_total is None else row_total + total
        numer = term if numer is None else numer + term
    return numer / row_total[..., None]


def reduce_scatter_line(x, axis):
    count = lax.axis_size(axis)
    width = x.shape[1] // count
    here = lax.axis_index(axis)

    def chunk(k):
        return x[:, k * width : (k + 1) * width].astype(jnp.float32)

    total = lax.dynamic_slice_in_dim(x, here * width, width, 1).astype(jnp.float32)
    from_below = {}
    from_above = {}
    for k in range(count - 1, 0, -1):
        carried = None
        for p in range(1, k + 1):
            send = chunk(k) if carried is None else chunk(k) + carried
            carried = lax.ppermute(send.astype(jnp.bfloat16), axis, [(p - 1, p)]).astype(jnp.float32)
        from_below[k] = carried
    for k in range(count - 1):
        carried = None
        for p in range(count - 2, k - 1, -1):
            send = chunk(k) if carried is None else chunk(k) + carried
            carried = lax.ppermute(send.astype(jnp.bfloat16), axis, [(p + 1, p)]).astype(jnp.float32)
        from_above[k] = carried
    for part in list(from_below.values()) + list(from_above.values()):
        total = total + part
    return total


def make_per_device(square):
    def gather_seq(x):
        if square:
            return gather_seq_square(x)
        return lax.all_gather(x, SEQ, axis=0, tiled=True)

    def per_device(query_proj, key_proj, value_proj, residual, out_weight):
        seg_rows = query_proj.shape[0]
        feat_width = query_proj.shape[1]
        heads_here = feat_width // HEAD_DIM
        seq_count = lax.axis_size("hi") * lax.axis_size("lo")
        chan_count = lax.axis_size("chan")
        segment = lax.axis_index("hi") * lax.axis_size("lo") + lax.axis_index("lo")
        score_scale = 1.0 / math.sqrt(HEAD_DIM)

        row_pos = segment * seg_rows + jnp.arange(seg_rows, dtype=jnp.int32)
        if square:
            def by_head(x):
                return x.reshape(seg_rows, heads_here, HEAD_DIM).transpose(1, 0, 2)

            key_blocks = gather_blocks_square(by_head(key_proj))
            value_blocks = gather_blocks_square(by_head(value_proj))
            chip = lax.axis_index("hi")
            core = lax.axis_index("lo")
            key_starts = [
                ((chip ^ (b // 2)) * 2 + (core ^ (b % 2))) * seg_rows for b in range(len(key_blocks))
            ]
            ratio = attention_by_head(by_head(query_proj), key_blocks, value_blocks, row_pos, key_starts)
        else:
            both = gather_seq(jnp.concatenate([key_proj, value_proj], axis=1))
            total_rows = both.shape[0]
            keys = both[:, :feat_width].reshape(total_rows, heads_here, HEAD_DIM)
            values = both[:, feat_width:].reshape(total_rows, heads_here, HEAD_DIM)
            key_pos = jnp.arange(total_rows, dtype=jnp.int32)
            queries = query_proj.reshape(seg_rows, heads_here, HEAD_DIM)
            scores = (
                jnp.einsum("qhd,khd->hqk", queries, keys, preferred_element_type=jnp.float32)
                * score_scale
            )
            allowed = (key_pos[None, :] <= row_pos[:, None])[None]
            scores = jnp.where(allowed, scores, -1e30)
            row_max = jnp.max(scores, axis=-1)
            weights = jnp.where(allowed, jnp.exp(scores - row_max[..., None]), 0.0)
            row_total = jnp.sum(weights, axis=-1)
            numer = jnp.einsum(
                "hqk,khd->hqd", weights.astype(jnp.bfloat16), values, preferred_element_type=jnp.float32
            )
            ratio = numer / row_total[..., None]
        local_context = ratio.transpose(1, 0, 2).reshape(seg_rows, feat_width).astype(jnp.bfloat16)

        gathered = gather_seq(local_context)
        group = seq_count // chan_count
        chunks = 2
        width = out_weight.shape[1] // chunks
        reduced = []
        for j in range(chunks):
            partial = jnp.dot(
                gathered, out_weight[:, j * width : (j + 1) * width], preferred_element_type=jnp.float32
            ).astype(jnp.bfloat16)
            by_row = lax.all_to_all(partial, SEQ, split_axis=0, concat_axis=1, tiled=True)
            if square:
                reduced.append(reduce_scatter_line(by_row, "chan"))
            else:
                reduced.append(
                    lax.psum_scatter(by_row, "chan", scatter_dimension=1, tiled=True).astype(
                        jnp.float32
                    )
                )
        ordered = jnp.concatenate(
            [part[:, b * width : (b + 1) * width] for b in range(group) for part in reduced], axis=1
        )
        return (residual.astype(jnp.float32) + ordered.astype(jnp.float32)).astype(jnp.bfloat16)

    return per_device


def solution(mesh):
    seq_size, chan_size = mesh.devices.shape
    n_lo = cores_per_chip_along_seq(mesh)
    split = Mesh(
        mesh.devices.reshape(seq_size // n_lo, n_lo, chan_size), ("hi", "lo", mesh.axis_names[1])
    )
    rows_cols = P(SEQ, "chan")
    placed = (rows_cols, rows_cols, rows_cols, rows_cols, P("chan", SEQ))
    return jax.shard_map(
        make_per_device(is_square_of_chips(mesh, n_lo)),
        mesh=split,
        in_specs=placed,
        out_specs=rows_cols,
        check_vma=False,
    )
```

```python
import math

import jax
import jax.numpy as jnp
import numpy as np
from jax import lax
from jax.sharding import Mesh
from jax.sharding import PartitionSpec as P

HEAD_DIM = 128
SEQ = ("hi", "lo")


def cores_per_chip_along_seq(mesh):
    column = mesh.devices[:, 0]
    first = tuple(column[0].coords)
    count = 1
    while count < len(column) and tuple(column[count].coords) == first:
        count += 1
    return count


def is_square_of_chips(mesh, n_lo):
    column = mesh.devices[::n_lo, 0]
    if n_lo != 2 or len(column) != 4:
        return False
    coords = [np.array(d.coords) for d in column]
    for i in range(4):
        for flip in (1, 2):
            if np.abs(coords[i] - coords[i ^ flip]).sum() != 1:
                return False
    return True


def swap(axis, flip, n):
    return [(i, i ^ flip) for i in range(n)]


def assemble(pieces, rows, width, dtype):
    out = jnp.zeros((len(pieces) * rows, width), dtype)
    for piece, slot in pieces:
        out = lax.dynamic_update_slice(out, piece, (slot * rows, 0))
    return out


def gather_seq_square(x):
    rows, width = x.shape
    half = rows // 2
    chip = lax.axis_index("hi")
    core = lax.axis_index("lo")
    from_x = lax.ppermute(x, "hi", swap("hi", 1, 4))
    from_y = lax.ppermute(x, "hi", swap("hi", 2, 4))
    diag = jnp.concatenate(
        [
            lax.ppermute(from_y[:half], "hi", swap("hi", 1, 4)),
            lax.ppermute(from_x[half:], "hi", swap("hi", 2, 4)),
        ],
        axis=0,
    )
    mine = [(x, chip), (from_x, chip ^ 1), (from_y, chip ^ 2), (diag, chip ^ 3)]
    pieces = []
    for block, source in mine:
        pieces.append((block, source * 2 + core))
        pieces.append((lax.ppermute(block, "lo", [(0, 1), (1, 0)]), source * 2 + (1 - core)))
    return assemble(pieces, rows, width, x.dtype)


def gather_blocks_square(x):
    half = x.shape[0] // 2
    from_x = lax.ppermute(x, "hi", swap("hi", 1, 4))
    from_y = lax.ppermute(x, "hi", swap("hi", 2, 4))
    diag = jnp.concatenate(
        [
            lax.ppermute(from_y[:half], "hi", swap("hi", 1, 4)),
            lax.ppermute(from_x[half:], "hi", swap("hi", 2, 4)),
        ],
        axis=0,
    )
    blocks = []
    for block in (x, from_x, from_y, diag):
        blocks.append(block)
        blocks.append(lax.ppermute(block, "lo", [(0, 1), (1, 0)]))
    return blocks


def attention_by_head(queries, key_blocks, value_blocks, row_pos, key_starts):
    score_scale = 1.0 / math.sqrt(HEAD_DIM)
    scores = []
    masks = []
    for keys, start in zip(key_blocks, key_starts):
        part = (
            jnp.einsum("hqd,hkd->hqk", queries, keys, preferred_element_type=jnp.float32)
            * score_scale
        )
        key_pos = start + jnp.arange(keys.shape[1], dtype=jnp.int32)
        allowed = (key_pos[None, :] <= row_pos[:, None])[None]
        scores.append(jnp.where(allowed, part, -1e30))
        masks.append(allowed)
    row_max = scores[0].max(axis=-1)
    for part in scores[1:]:
        row_max = jnp.maximum(row_max, part.max(axis=-1))
    row_total = None
    numer = None
    for part, allowed, values in zip(scores, masks, value_blocks):
        weights = jnp.where(allowed, jnp.exp(part - row_max[..., None]), 0.0)
        total = jnp.sum(weights, axis=-1)
        term = jnp.einsum(
            "hqk,hkd->hqd", weights.astype(jnp.bfloat16), values, preferred_element_type=jnp.float32
        )
        row_total = total if row_total is None else row_total + total
        numer = term if numer is None else numer + term
    return numer / row_total[..., None]


def make_per_device(square):
    def gather_seq(x):
        if square:
            return gather_seq_square(x)
        return lax.all_gather(x, SEQ, axis=0, tiled=True)

    def per_device(query_proj, key_proj, value_proj, residual, out_weight):
        seg_rows = query_proj.shape[0]
        feat_width = query_proj.shape[1]
        heads_here = feat_width // HEAD_DIM
        seq_count = lax.axis_size("hi") * lax.axis_size("lo")
        chan_count = lax.axis_size("chan")
        segment = lax.axis_index("hi") * lax.axis_size("lo") + lax.axis_index("lo")
        score_scale = 1.0 / math.sqrt(HEAD_DIM)

        row_pos = segment * seg_rows + jnp.arange(seg_rows, dtype=jnp.int32)
        if square:
            def by_head(x):
                return x.reshape(seg_rows, heads_here, HEAD_DIM).transpose(1, 0, 2)

            key_blocks = gather_blocks_square(by_head(key_proj))
            value_blocks = gather_blocks_square(by_head(value_proj))
            chip = lax.axis_index("hi")
            core = lax.axis_index("lo")
            key_starts = [
                ((chip ^ (b // 2)) * 2 + (core ^ (b % 2))) * seg_rows for b in range(len(key_blocks))
            ]
            ratio = attention_by_head(by_head(query_proj), key_blocks, value_blocks, row_pos, key_starts)
        else:
            both = gather_seq(jnp.concatenate([key_proj, value_proj], axis=1))
            total_rows = both.shape[0]
            keys = both[:, :feat_width].reshape(total_rows, heads_here, HEAD_DIM)
            values = both[:, feat_width:].reshape(total_rows, heads_here, HEAD_DIM)
            key_pos = jnp.arange(total_rows, dtype=jnp.int32)
            queries = query_proj.reshape(seg_rows, heads_here, HEAD_DIM)
            scores = (
                jnp.einsum("qhd,khd->hqk", queries, keys, preferred_element_type=jnp.float32)
                * score_scale
            )
            allowed = (key_pos[None, :] <= row_pos[:, None])[None]
            scores = jnp.where(allowed, scores, -1e30)
            row_max = jnp.max(scores, axis=-1)
            weights = jnp.where(allowed, jnp.exp(scores - row_max[..., None]), 0.0)
            row_total = jnp.sum(weights, axis=-1)
            numer = jnp.einsum(
                "hqk,khd->hqd", weights.astype(jnp.bfloat16), values, preferred_element_type=jnp.float32
            )
            ratio = numer / row_total[..., None]
        local_context = ratio.transpose(1, 0, 2).reshape(seg_rows, feat_width).astype(jnp.bfloat16)

        if square:
            chip = lax.axis_index("hi")
            core = lax.axis_index("lo")
            blocks = gather_blocks_square(local_context)
            width = out_weight.shape[1]
            by_row = jnp.zeros((seg_rows, seq_count * width), jnp.bfloat16)
            for b, block in enumerate(blocks):
                r, t = b // 2, b % 2
                partial = jnp.dot(block, out_weight, preferred_element_type=jnp.float32).astype(
                    jnp.bfloat16
                )
                if b:
                    pairs = [(h * 2 + l, (h ^ r) * 2 + (l ^ t)) for h in range(4) for l in range(2)]
                    partial = lax.ppermute(partial, SEQ, pairs)
                source = (chip ^ r) * 2 + (core ^ t)
                by_row = lax.dynamic_update_slice(by_row, partial, (0, source * width))
            ordered = lax.psum_scatter(by_row, "chan", scatter_dimension=1, tiled=True)
            return (residual.astype(jnp.float32) + ordered.astype(jnp.float32)).astype(jnp.bfloat16)
        gathered = gather_seq(local_context)
        group = seq_count // chan_count
        chunks = 2
        width = out_weight.shape[1] // chunks
        reduced = []
        for j in range(chunks):
            partial = jnp.dot(
                gathered, out_weight[:, j * width : (j + 1) * width], preferred_element_type=jnp.float32
            ).astype(jnp.bfloat16)
            by_row = lax.all_to_all(partial, SEQ, split_axis=0, concat_axis=1, tiled=True)
            reduced.append(
                lax.psum_scatter(by_row, "chan", scatter_dimension=1, tiled=True)
            )
        ordered = jnp.concatenate(
            [part[:, b * width : (b + 1) * width] for b in range(group) for part in reduced], axis=1
        )
        return (residual.astype(jnp.float32) + ordered.astype(jnp.float32)).astype(jnp.bfloat16)

    return per_device


def solution(mesh):
    seq_size, chan_size = mesh.devices.shape
    n_lo = cores_per_chip_along_seq(mesh)
    split = Mesh(
        mesh.devices.reshape(seq_size // n_lo, n_lo, chan_size), ("hi", "lo", mesh.axis_names[1])
    )
    rows_cols = P(SEQ, "chan")
    placed = (rows_cols, rows_cols, rows_cols, rows_cols, P("chan", SEQ))
    return jax.shard_map(
        make_per_device(is_square_of_chips(mesh, n_lo)),
        mesh=split,
        in_specs=placed,
        out_specs=rows_cols,
        check_vma=False,
    )
```

```python
import math

import jax
import jax.numpy as jnp
import numpy as np
from jax import lax
from jax.sharding import Mesh
from jax.sharding import PartitionSpec as P

HEAD_DIM = 128
SEQ = ("hi", "lo")


def cores_per_chip_along_seq(mesh):
    column = mesh.devices[:, 0]
    first = tuple(column[0].coords)
    count = 1
    while count < len(column) and tuple(column[count].coords) == first:
        count += 1
    return count


def is_square_of_chips(mesh, n_lo):
    column = mesh.devices[::n_lo, 0]
    if n_lo != 2 or len(column) != 4:
        return False
    coords = [np.array(d.coords) for d in column]
    for i in range(4):
        for flip in (1, 2):
            if np.abs(coords[i] - coords[i ^ flip]).sum() != 1:
                return False
    return True


def swap(axis, flip, n):
    return [(i, i ^ flip) for i in range(n)]


def assemble(pieces, rows, width, dtype):
    out = jnp.zeros((len(pieces) * rows, width), dtype)
    for piece, slot in pieces:
        out = lax.dynamic_update_slice(out, piece, (slot * rows, 0))
    return out


def gather_seq_square(x):
    rows, width = x.shape
    half = rows // 2
    chip = lax.axis_index("hi")
    core = lax.axis_index("lo")
    from_x = lax.ppermute(x, "hi", swap("hi", 1, 4))
    from_y = lax.ppermute(x, "hi", swap("hi", 2, 4))
    diag = jnp.concatenate(
        [
            lax.ppermute(from_y[:half], "hi", swap("hi", 1, 4)),
            lax.ppermute(from_x[half:], "hi", swap("hi", 2, 4)),
        ],
        axis=0,
    )
    mine = [(x, chip), (from_x, chip ^ 1), (from_y, chip ^ 2), (diag, chip ^ 3)]
    pieces = []
    for block, source in mine:
        pieces.append((block, source * 2 + core))
        pieces.append((lax.ppermute(block, "lo", [(0, 1), (1, 0)]), source * 2 + (1 - core)))
    return assemble(pieces, rows, width, x.dtype)


def gather_blocks_square(x):
    half = x.shape[0] // 2
    from_x = lax.ppermute(x, "hi", swap("hi", 1, 4))
    from_y = lax.ppermute(x, "hi", swap("hi", 2, 4))
    diag = jnp.concatenate(
        [
            lax.ppermute(from_y[:half], "hi", swap("hi", 1, 4)),
            lax.ppermute(from_x[half:], "hi", swap("hi", 2, 4)),
        ],
        axis=0,
    )
    blocks = []
    for block in (x, from_x, from_y, diag):
        blocks.append(block)
        blocks.append(lax.ppermute(block, "lo", [(0, 1), (1, 0)]))
    return blocks


def attention_by_head(queries, key_blocks, value_blocks, row_pos, key_starts):
    score_scale = 1.0 / math.sqrt(HEAD_DIM)
    scores = []
    masks = []
    for keys, start in zip(key_blocks, key_starts):
        part = (
            jnp.einsum("hqd,hkd->hqk", queries, keys, preferred_element_type=jnp.float32)
            * score_scale
        )
        key_pos = start + jnp.arange(keys.shape[1], dtype=jnp.int32)
        allowed = (key_pos[None, :] <= row_pos[:, None])[None]
        scores.append(jnp.where(allowed, part, -1e30))
        masks.append(allowed)
    row_max = scores[0].max(axis=-1)
    for part in scores[1:]:
        row_max = jnp.maximum(row_max, part.max(axis=-1))
    row_total = None
    numer = None
    for part, allowed, values in zip(scores, masks, value_blocks):
        weights = jnp.where(allowed, jnp.exp(part - row_max[..., None]), 0.0)
        total = jnp.sum(weights, axis=-1)
        term = jnp.einsum(
            "hqk,hkd->hqd", weights.astype(jnp.bfloat16), values, preferred_element_type=jnp.float32
        )
        row_total = total if row_total is None else row_total + total
        numer = term if numer is None else numer + term
    return numer / row_total[..., None]


def make_per_device(square):
    def gather_seq(x):
        if square:
            return gather_seq_square(x)
        return lax.all_gather(x, SEQ, axis=0, tiled=True)

    def per_device(query_proj, key_proj, value_proj, residual, out_weight):
        seg_rows = query_proj.shape[0]
        feat_width = query_proj.shape[1]
        heads_here = feat_width // HEAD_DIM
        seq_count = lax.axis_size("hi") * lax.axis_size("lo")
        chan_count = lax.axis_size("chan")
        segment = lax.axis_index("hi") * lax.axis_size("lo") + lax.axis_index("lo")
        score_scale = 1.0 / math.sqrt(HEAD_DIM)

        row_pos = segment * seg_rows + jnp.arange(seg_rows, dtype=jnp.int32)
        if square:
            def by_head(x):
                return x.reshape(seg_rows, heads_here, HEAD_DIM).transpose(1, 0, 2)

            key_blocks = gather_blocks_square(by_head(key_proj))
            value_blocks = gather_blocks_square(by_head(value_proj))
            chip = lax.axis_index("hi")
            core = lax.axis_index("lo")
            key_starts = [
                ((chip ^ (b // 2)) * 2 + (core ^ (b % 2))) * seg_rows for b in range(len(key_blocks))
            ]
            ratio = attention_by_head(by_head(query_proj), key_blocks, value_blocks, row_pos, key_starts)
        else:
            both = gather_seq(jnp.concatenate([key_proj, value_proj], axis=1))
            total_rows = both.shape[0]
            keys = both[:, :feat_width].reshape(total_rows, heads_here, HEAD_DIM)
            values = both[:, feat_width:].reshape(total_rows, heads_here, HEAD_DIM)
            key_pos = jnp.arange(total_rows, dtype=jnp.int32)
            queries = query_proj.reshape(seg_rows, heads_here, HEAD_DIM)
            scores = (
                jnp.einsum("qhd,khd->hqk", queries, keys, preferred_element_type=jnp.float32)
                * score_scale
            )
            allowed = (key_pos[None, :] <= row_pos[:, None])[None]
            scores = jnp.where(allowed, scores, -1e30)
            row_max = jnp.max(scores, axis=-1)
            weights = jnp.where(allowed, jnp.exp(scores - row_max[..., None]), 0.0)
            row_total = jnp.sum(weights, axis=-1)
            numer = jnp.einsum(
                "hqk,khd->hqd", weights.astype(jnp.bfloat16), values, preferred_element_type=jnp.float32
            )
            ratio = numer / row_total[..., None]
        local_context = ratio.transpose(1, 0, 2).reshape(seg_rows, feat_width).astype(jnp.bfloat16)

        if square:
            chip = lax.axis_index("hi")
            core = lax.axis_index("lo")
            blocks = gather_blocks_square(local_context)
            width = out_weight.shape[1]
            half = seg_rows // 2
            reduced = []
            for h in range(2):
                by_row = jnp.zeros((half, seq_count * width), jnp.bfloat16)
                for b, block in enumerate(blocks):
                    r, t = b // 2, b % 2
                    partial = jnp.dot(
                        block[h * half : (h + 1) * half], out_weight, preferred_element_type=jnp.float32
                    ).astype(jnp.bfloat16)
                    if b:
                        pairs = [(i * 2 + l, (i ^ r) * 2 + (l ^ t)) for i in range(4) for l in range(2)]
                        partial = lax.ppermute(partial, SEQ, pairs)
                    source = (chip ^ r) * 2 + (core ^ t)
                    by_row = lax.dynamic_update_slice(by_row, partial, (0, source * width))
                reduced.append(lax.psum_scatter(by_row, "chan", scatter_dimension=1, tiled=True))
            ordered = jnp.concatenate(reduced, axis=0)
            return (residual.astype(jnp.float32) + ordered.astype(jnp.float32)).astype(jnp.bfloat16)
        gathered = gather_seq(local_context)
        group = seq_count // chan_count
        chunks = 2
        width = out_weight.shape[1] // chunks
        reduced = []
        for j in range(chunks):
            partial = jnp.dot(
                gathered, out_weight[:, j * width : (j + 1) * width], preferred_element_type=jnp.float32
            ).astype(jnp.bfloat16)
            by_row = lax.all_to_all(partial, SEQ, split_axis=0, concat_axis=1, tiled=True)
            reduced.append(
                lax.psum_scatter(by_row, "chan", scatter_dimension=1, tiled=True)
            )
        ordered = jnp.concatenate(
            [part[:, b * width : (b + 1) * width] for b in range(group) for part in reduced], axis=1
        )
        return (residual.astype(jnp.float32) + ordered.astype(jnp.float32)).astype(jnp.bfloat16)

    return per_device


def solution(mesh):
    seq_size, chan_size = mesh.devices.shape
    n_lo = cores_per_chip_along_seq(mesh)
    split = Mesh(
        mesh.devices.reshape(seq_size // n_lo, n_lo, chan_size), ("hi", "lo", mesh.axis_names[1])
    )
    rows_cols = P(SEQ, "chan")
    placed = (rows_cols, rows_cols, rows_cols, rows_cols, P("chan", SEQ))
    return jax.shard_map(
        make_per_device(is_square_of_chips(mesh, n_lo)),
        mesh=split,
        in_specs=placed,
        out_specs=rows_cols,
        check_vma=False,
    )
```

```python
import math

import jax
import jax.numpy as jnp
import numpy as np
from jax import lax
from jax.sharding import Mesh
from jax.sharding import PartitionSpec as P

HEAD_DIM = 128
SEQ = ("hi", "lo")


def cores_per_chip_along_seq(mesh):
    column = mesh.devices[:, 0]
    first = tuple(column[0].coords)
    count = 1
    while count < len(column) and tuple(column[count].coords) == first:
        count += 1
    return count


def is_square_of_chips(mesh, n_lo):
    column = mesh.devices[::n_lo, 0]
    if n_lo != 2 or len(column) != 4:
        return False
    coords = [np.array(d.coords) for d in column]
    for i in range(4):
        for flip in (1, 2):
            if np.abs(coords[i] - coords[i ^ flip]).sum() != 1:
                return False
    return True


def swap(axis, flip, n):
    return [(i, i ^ flip) for i in range(n)]


def assemble(pieces, rows, width, dtype):
    out = jnp.zeros((len(pieces) * rows, width), dtype)
    for piece, slot in pieces:
        out = lax.dynamic_update_slice(out, piece, (slot * rows, 0))
    return out


def gather_seq_square(x):
    rows, width = x.shape
    half = rows // 2
    chip = lax.axis_index("hi")
    core = lax.axis_index("lo")
    from_x = lax.ppermute(x, "hi", swap("hi", 1, 4))
    from_y = lax.ppermute(x, "hi", swap("hi", 2, 4))
    diag = jnp.concatenate(
        [
            lax.ppermute(from_y[:half], "hi", swap("hi", 1, 4)),
            lax.ppermute(from_x[half:], "hi", swap("hi", 2, 4)),
        ],
        axis=0,
    )
    mine = [(x, chip), (from_x, chip ^ 1), (from_y, chip ^ 2), (diag, chip ^ 3)]
    pieces = []
    for block, source in mine:
        pieces.append((block, source * 2 + core))
        pieces.append((lax.ppermute(block, "lo", [(0, 1), (1, 0)]), source * 2 + (1 - core)))
    return assemble(pieces, rows, width, x.dtype)


def gather_blocks_square(x):
    half = x.shape[0] // 2
    from_x = lax.ppermute(x, "hi", swap("hi", 1, 4))
    from_y = lax.ppermute(x, "hi", swap("hi", 2, 4))
    diag = jnp.concatenate(
        [
            lax.ppermute(from_y[:half], "hi", swap("hi", 1, 4)),
            lax.ppermute(from_x[half:], "hi", swap("hi", 2, 4)),
        ],
        axis=0,
    )
    blocks = []
    for block in (x, from_x, from_y, diag):
        blocks.append(block)
        blocks.append(lax.ppermute(block, "lo", [(0, 1), (1, 0)]))
    return blocks


def attention_by_head(queries, key_blocks, value_blocks, row_pos, key_starts):
    score_scale = 1.0 / math.sqrt(HEAD_DIM)
    scores = []
    masks = []
    for keys, start in zip(key_blocks, key_starts):
        part = (
            jnp.einsum("hqd,hkd->hqk", queries, keys, preferred_element_type=jnp.float32)
            * score_scale
        )
        key_pos = start + jnp.arange(keys.shape[1], dtype=jnp.int32)
        allowed = (key_pos[None, :] <= row_pos[:, None])[None]
        scores.append(jnp.where(allowed, part, -1e30))
        masks.append(allowed)
    row_max = scores[0].max(axis=-1)
    for part in scores[1:]:
        row_max = jnp.maximum(row_max, part.max(axis=-1))
    row_total = None
    numer = None
    for part, allowed, values in zip(scores, masks, value_blocks):
        weights = jnp.where(allowed, jnp.exp(part - row_max[..., None]), 0.0)
        total = jnp.sum(weights, axis=-1)
        term = jnp.einsum(
            "hqk,hkd->hqd", weights.astype(jnp.bfloat16), values, preferred_element_type=jnp.float32
        )
        row_total = total if row_total is None else row_total + total
        numer = term if numer is None else numer + term
    return numer / row_total[..., None]


def make_per_device(square):
    def gather_seq(x):
        if square:
            return gather_seq_square(x)
        return lax.all_gather(x, SEQ, axis=0, tiled=True)

    def per_device(query_proj, key_proj, value_proj, residual, out_weight):
        seg_rows = query_proj.shape[0]
        feat_width = query_proj.shape[1]
        heads_here = feat_width // HEAD_DIM
        seq_count = lax.axis_size("hi") * lax.axis_size("lo")
        chan_count = lax.axis_size("chan")
        segment = lax.axis_index("hi") * lax.axis_size("lo") + lax.axis_index("lo")
        score_scale = 1.0 / math.sqrt(HEAD_DIM)

        row_pos = segment * seg_rows + jnp.arange(seg_rows, dtype=jnp.int32)
        if square:
            def by_head(x):
                return x.reshape(seg_rows, heads_here, HEAD_DIM).transpose(1, 0, 2)

            both = gather_blocks_square(jnp.stack([by_head(key_proj), by_head(value_proj)]))
            key_blocks = [block[0] for block in both]
            value_blocks = [block[1] for block in both]
            chip = lax.axis_index("hi")
            core = lax.axis_index("lo")
            key_starts = [
                ((chip ^ (b // 2)) * 2 + (core ^ (b % 2))) * seg_rows for b in range(len(key_blocks))
            ]
            ratio = attention_by_head(by_head(query_proj), key_blocks, value_blocks, row_pos, key_starts)
        else:
            both = gather_seq(jnp.concatenate([key_proj, value_proj], axis=1))
            total_rows = both.shape[0]
            keys = both[:, :feat_width].reshape(total_rows, heads_here, HEAD_DIM)
            values = both[:, feat_width:].reshape(total_rows, heads_here, HEAD_DIM)
            key_pos = jnp.arange(total_rows, dtype=jnp.int32)
            queries = query_proj.reshape(seg_rows, heads_here, HEAD_DIM)
            scores = (
                jnp.einsum("qhd,khd->hqk", queries, keys, preferred_element_type=jnp.float32)
                * score_scale
            )
            allowed = (key_pos[None, :] <= row_pos[:, None])[None]
            scores = jnp.where(allowed, scores, -1e30)
            row_max = jnp.max(scores, axis=-1)
            weights = jnp.where(allowed, jnp.exp(scores - row_max[..., None]), 0.0)
            row_total = jnp.sum(weights, axis=-1)
            numer = jnp.einsum(
                "hqk,khd->hqd", weights.astype(jnp.bfloat16), values, preferred_element_type=jnp.float32
            )
            ratio = numer / row_total[..., None]
        local_context = ratio.transpose(1, 0, 2).reshape(seg_rows, feat_width).astype(jnp.bfloat16)

        if square:
            chip = lax.axis_index("hi")
            core = lax.axis_index("lo")
            blocks = gather_blocks_square(local_context)
            width = out_weight.shape[1]
            by_row = jnp.zeros((seg_rows, seq_count * width), jnp.bfloat16)
            for b, block in enumerate(blocks):
                r, t = b // 2, b % 2
                partial = jnp.dot(block, out_weight, preferred_element_type=jnp.float32).astype(
                    jnp.bfloat16
                )
                if b:
                    pairs = [(h * 2 + l, (h ^ r) * 2 + (l ^ t)) for h in range(4) for l in range(2)]
                    partial = lax.ppermute(partial, SEQ, pairs)
                source = (chip ^ r) * 2 + (core ^ t)
                by_row = lax.dynamic_update_slice(by_row, partial, (0, source * width))
            ordered = lax.psum_scatter(by_row, "chan", scatter_dimension=1, tiled=True)
            return (residual.astype(jnp.float32) + ordered.astype(jnp.float32)).astype(jnp.bfloat16)
        gathered = gather_seq(local_context)
        group = seq_count // chan_count
        chunks = 2
        width = out_weight.shape[1] // chunks
        reduced = []
        for j in range(chunks):
            partial = jnp.dot(
                gathered, out_weight[:, j * width : (j + 1) * width], preferred_element_type=jnp.float32
            ).astype(jnp.bfloat16)
            by_row = lax.all_to_all(partial, SEQ, split_axis=0, concat_axis=1, tiled=True)
            reduced.append(
                lax.psum_scatter(by_row, "chan", scatter_dimension=1, tiled=True)
            )
        ordered = jnp.concatenate(
            [part[:, b * width : (b + 1) * width] for b in range(group) for part in reduced], axis=1
        )
        return (residual.astype(jnp.float32) + ordered.astype(jnp.float32)).astype(jnp.bfloat16)

    return per_device


def solution(mesh):
    seq_size, chan_size = mesh.devices.shape
    n_lo = cores_per_chip_along_seq(mesh)
    split = Mesh(
        mesh.devices.reshape(seq_size // n_lo, n_lo, chan_size), ("hi", "lo", mesh.axis_names[1])
    )
    rows_cols = P(SEQ, "chan")
    placed = (rows_cols, rows_cols, rows_cols, rows_cols, P("chan", SEQ))
    return jax.shard_map(
        make_per_device(is_square_of_chips(mesh, n_lo)),
        mesh=split,
        in_specs=placed,
        out_specs=rows_cols,
        check_vma=False,
    )
```

```python
import math

import jax
import jax.numpy as jnp
import numpy as np
from jax import lax
from jax.sharding import Mesh
from jax.sharding import PartitionSpec as P

HEAD_DIM = 128
SEQ = ("hi", "lo")


def cores_per_chip_along_seq(mesh):
    column = mesh.devices[:, 0]
    first = tuple(column[0].coords)
    count = 1
    while count < len(column) and tuple(column[count].coords) == first:
        count += 1
    return count


def is_square_of_chips(mesh, n_lo):
    column = mesh.devices[::n_lo, 0]
    if n_lo != 2 or len(column) != 4:
        return False
    coords = [np.array(d.coords) for d in column]
    for i in range(4):
        for flip in (1, 2):
            if np.abs(coords[i] - coords[i ^ flip]).sum() != 1:
                return False
    return True


def swap(axis, flip, n):
    return [(i, i ^ flip) for i in range(n)]


def assemble(pieces, rows, width, dtype):
    out = jnp.zeros((len(pieces) * rows, width), dtype)
    for piece, slot in pieces:
        out = lax.dynamic_update_slice(out, piece, (slot * rows, 0))
    return out


def gather_seq_square(x):
    rows, width = x.shape
    half = rows // 2
    chip = lax.axis_index("hi")
    core = lax.axis_index("lo")
    from_x = lax.ppermute(x, "hi", swap("hi", 1, 4))
    from_y = lax.ppermute(x, "hi", swap("hi", 2, 4))
    diag = jnp.concatenate(
        [
            lax.ppermute(from_y[:half], "hi", swap("hi", 1, 4)),
            lax.ppermute(from_x[half:], "hi", swap("hi", 2, 4)),
        ],
        axis=0,
    )
    mine = [(x, chip), (from_x, chip ^ 1), (from_y, chip ^ 2), (diag, chip ^ 3)]
    pieces = []
    for block, source in mine:
        pieces.append((block, source * 2 + core))
        pieces.append((lax.ppermute(block, "lo", [(0, 1), (1, 0)]), source * 2 + (1 - core)))
    return assemble(pieces, rows, width, x.dtype)


def gather_blocks_square(x):
    half = x.shape[0] // 2
    from_x = lax.ppermute(x, "hi", swap("hi", 1, 4))
    from_y = lax.ppermute(x, "hi", swap("hi", 2, 4))
    diag = jnp.concatenate(
        [
            lax.ppermute(from_y[:half], "hi", swap("hi", 1, 4)),
            lax.ppermute(from_x[half:], "hi", swap("hi", 2, 4)),
        ],
        axis=0,
    )
    blocks = []
    for block in (x, from_x, from_y, diag):
        blocks.append(block)
        blocks.append(lax.ppermute(block, "lo", [(0, 1), (1, 0)]))
    return blocks


def attention_by_head(queries, key_blocks, value_blocks, row_pos, key_starts):
    score_scale = 1.0 / math.sqrt(HEAD_DIM)
    row_max = None
    for keys, values, start in zip(key_blocks, value_blocks, key_starts):
        part = (
            jnp.einsum("hqd,hkd->hqk", queries, keys, preferred_element_type=jnp.float32)
            * score_scale
        )
        key_pos = start + jnp.arange(keys.shape[1], dtype=jnp.int32)
        allowed = (key_pos[None, :] <= row_pos[:, None])[None]
        part = jnp.where(allowed, part, -1e30)
        if row_max is None:
            new_max = jnp.max(part, axis=-1)
        else:
            new_max = jnp.maximum(row_max, jnp.max(part, axis=-1))
        weights = jnp.where(allowed, jnp.exp(part - new_max[..., None]), 0.0)
        term = jnp.einsum(
            "hqk,hkd->hqd", weights.astype(jnp.bfloat16), values, preferred_element_type=jnp.float32
        )
        if row_max is None:
            row_total = jnp.sum(weights, axis=-1)
            numer = term
        else:
            factor = jnp.exp(row_max - new_max)
            row_total = row_total * factor + jnp.sum(weights, axis=-1)
            numer = numer * factor[..., None] + term
        row_max = new_max
    return numer / row_total[..., None]


def make_per_device(square):
    def gather_seq(x):
        if square:
            return gather_seq_square(x)
        return lax.all_gather(x, SEQ, axis=0, tiled=True)

    def per_device(query_proj, key_proj, value_proj, residual, out_weight):
        seg_rows = query_proj.shape[0]
        feat_width = query_proj.shape[1]
        heads_here = feat_width // HEAD_DIM
        seq_count = lax.axis_size("hi") * lax.axis_size("lo")
        chan_count = lax.axis_size("chan")
        segment = lax.axis_index("hi") * lax.axis_size("lo") + lax.axis_index("lo")
        score_scale = 1.0 / math.sqrt(HEAD_DIM)

        row_pos = segment * seg_rows + jnp.arange(seg_rows, dtype=jnp.int32)
        if square:
            def by_head(x):
                return x.reshape(seg_rows, heads_here, HEAD_DIM).transpose(1, 0, 2)

            key_blocks = gather_blocks_square(by_head(key_proj))
            value_blocks = gather_blocks_square(by_head(value_proj))
            chip = lax.axis_index("hi")
            core = lax.axis_index("lo")
            key_starts = [
                ((chip ^ (b // 2)) * 2 + (core ^ (b % 2))) * seg_rows for b in range(len(key_blocks))
            ]
            ratio = attention_by_head(by_head(query_proj), key_blocks, value_blocks, row_pos, key_starts)
        else:
            both = gather_seq(jnp.concatenate([key_proj, value_proj], axis=1))
            total_rows = both.shape[0]
            keys = both[:, :feat_width].reshape(total_rows, heads_here, HEAD_DIM)
            values = both[:, feat_width:].reshape(total_rows, heads_here, HEAD_DIM)
            key_pos = jnp.arange(total_rows, dtype=jnp.int32)
            queries = query_proj.reshape(seg_rows, heads_here, HEAD_DIM)
            scores = (
                jnp.einsum("qhd,khd->hqk", queries, keys, preferred_element_type=jnp.float32)
                * score_scale
            )
            allowed = (key_pos[None, :] <= row_pos[:, None])[None]
            scores = jnp.where(allowed, scores, -1e30)
            row_max = jnp.max(scores, axis=-1)
            weights = jnp.where(allowed, jnp.exp(scores - row_max[..., None]), 0.0)
            row_total = jnp.sum(weights, axis=-1)
            numer = jnp.einsum(
                "hqk,khd->hqd", weights.astype(jnp.bfloat16), values, preferred_element_type=jnp.float32
            )
            ratio = numer / row_total[..., None]
        local_context = ratio.transpose(1, 0, 2).reshape(seg_rows, feat_width).astype(jnp.bfloat16)

        if square:
            chip = lax.axis_index("hi")
            core = lax.axis_index("lo")
            blocks = gather_blocks_square(local_context)
            width = out_weight.shape[1]
            by_row = jnp.zeros((seg_rows, seq_count * width), jnp.bfloat16)
            for b, block in enumerate(blocks):
                r, t = b // 2, b % 2
                partial = jnp.dot(block, out_weight, preferred_element_type=jnp.float32).astype(
                    jnp.bfloat16
                )
                if b:
                    pairs = [(h * 2 + l, (h ^ r) * 2 + (l ^ t)) for h in range(4) for l in range(2)]
                    partial = lax.ppermute(partial, SEQ, pairs)
                source = (chip ^ r) * 2 + (core ^ t)
                by_row = lax.dynamic_update_slice(by_row, partial, (0, source * width))
            ordered = lax.psum_scatter(by_row, "chan", scatter_dimension=1, tiled=True)
            return (residual.astype(jnp.float32) + ordered.astype(jnp.float32)).astype(jnp.bfloat16)
        gathered = gather_seq(local_context)
        group = seq_count // chan_count
        chunks = 2
        width = out_weight.shape[1] // chunks
        reduced = []
        for j in range(chunks):
            partial = jnp.dot(
                gathered, out_weight[:, j * width : (j + 1) * width], preferred_element_type=jnp.float32
            ).astype(jnp.bfloat16)
            by_row = lax.all_to_all(partial, SEQ, split_axis=0, concat_axis=1, tiled=True)
            reduced.append(
                lax.psum_scatter(by_row, "chan", scatter_dimension=1, tiled=True)
            )
        ordered = jnp.concatenate(
            [part[:, b * width : (b + 1) * width] for b in range(group) for part in reduced], axis=1
        )
        return (residual.astype(jnp.float32) + ordered.astype(jnp.float32)).astype(jnp.bfloat16)

    return per_device


def solution(mesh):
    seq_size, chan_size = mesh.devices.shape
    n_lo = cores_per_chip_along_seq(mesh)
    split = Mesh(
        mesh.devices.reshape(seq_size // n_lo, n_lo, chan_size), ("hi", "lo", mesh.axis_names[1])
    )
    rows_cols = P(SEQ, "chan")
    placed = (rows_cols, rows_cols, rows_cols, rows_cols, P("chan", SEQ))
    return jax.shard_map(
        make_per_device(is_square_of_chips(mesh, n_lo)),
        mesh=split,
        in_specs=placed,
        out_specs=rows_cols,
        check_vma=False,
    )
```

```python
import math

import jax
import jax.numpy as jnp
import numpy as np
from jax import lax
from jax.sharding import Mesh
from jax.sharding import PartitionSpec as P

HEAD_DIM = 128
SEQ = ("hi", "lo")


def cores_per_chip_along_seq(mesh):
    column = mesh.devices[:, 0]
    first = tuple(column[0].coords)
    count = 1
    while count < len(column) and tuple(column[count].coords) == first:
        count += 1
    return count


def is_square_of_chips(mesh, n_lo):
    column = mesh.devices[::n_lo, 0]
    if n_lo != 2 or len(column) != 4:
        return False
    coords = [np.array(d.coords) for d in column]
    for i in range(4):
        for flip in (1, 2):
            if np.abs(coords[i] - coords[i ^ flip]).sum() != 1:
                return False
    return True


def swap(axis, flip, n):
    return [(i, i ^ flip) for i in range(n)]


def assemble(pieces, rows, width, dtype):
    out = jnp.zeros((len(pieces) * rows, width), dtype)
    for piece, slot in pieces:
        out = lax.dynamic_update_slice(out, piece, (slot * rows, 0))
    return out


def gather_seq_square(x):
    rows, width = x.shape
    half = rows // 2
    chip = lax.axis_index("hi")
    core = lax.axis_index("lo")
    from_x = lax.ppermute(x, "hi", swap("hi", 1, 4))
    from_y = lax.ppermute(x, "hi", swap("hi", 2, 4))
    diag = jnp.concatenate(
        [
            lax.ppermute(from_y[:half], "hi", swap("hi", 1, 4)),
            lax.ppermute(from_x[half:], "hi", swap("hi", 2, 4)),
        ],
        axis=0,
    )
    mine = [(x, chip), (from_x, chip ^ 1), (from_y, chip ^ 2), (diag, chip ^ 3)]
    pieces = []
    for block, source in mine:
        pieces.append((block, source * 2 + core))
        pieces.append((lax.ppermute(block, "lo", [(0, 1), (1, 0)]), source * 2 + (1 - core)))
    return assemble(pieces, rows, width, x.dtype)


def gather_blocks_square(x):
    half = x.shape[0] // 2
    from_x = lax.ppermute(x, "hi", swap("hi", 1, 4))
    from_y = lax.ppermute(x, "hi", swap("hi", 2, 4))
    diag = jnp.concatenate(
        [
            lax.ppermute(from_y[:half], "hi", swap("hi", 1, 4)),
            lax.ppermute(from_x[half:], "hi", swap("hi", 2, 4)),
        ],
        axis=0,
    )
    blocks = []
    for block in (x, from_x, from_y, diag):
        blocks.append(block)
        blocks.append(lax.ppermute(block, "lo", [(0, 1), (1, 0)]))
    return blocks


def attention_by_head(queries, key_blocks, value_blocks, row_pos, key_starts):
    score_scale = 1.0 / math.sqrt(HEAD_DIM)
    scores = []
    masks = []
    for keys, start in zip(key_blocks, key_starts):
        part = (
            jnp.einsum("hqd,hkd->hqk", queries, keys, preferred_element_type=jnp.float32)
            * score_scale
        )
        key_pos = start + jnp.arange(keys.shape[1], dtype=jnp.int32)
        allowed = (key_pos[None, :] <= row_pos[:, None])[None]
        scores.append(jnp.where(allowed, part, -1e30))
        masks.append(allowed)
    row_max = scores[0].max(axis=-1)
    for part in scores[1:]:
        row_max = jnp.maximum(row_max, part.max(axis=-1))
    row_total = None
    numer = None
    for part, allowed, values in zip(scores, masks, value_blocks):
        weights = jnp.where(allowed, jnp.exp(part - row_max[..., None]), 0.0)
        total = jnp.sum(weights, axis=-1)
        term = jnp.einsum(
            "hqk,hkd->hqd", weights.astype(jnp.bfloat16), values, preferred_element_type=jnp.float32
        )
        row_total = total if row_total is None else row_total + total
        numer = term if numer is None else numer + term
    return numer / row_total[..., None]


def make_per_device(square):
    def gather_seq(x):
        if square:
            return gather_seq_square(x)
        return lax.all_gather(x, SEQ, axis=0, tiled=True)

    def per_device(query_proj, key_proj, value_proj, residual, out_weight):
        seg_rows = query_proj.shape[0]
        feat_width = query_proj.shape[1]
        heads_here = feat_width // HEAD_DIM
        seq_count = lax.axis_size("hi") * lax.axis_size("lo")
        chan_count = lax.axis_size("chan")
        segment = lax.axis_index("hi") * lax.axis_size("lo") + lax.axis_index("lo")
        score_scale = 1.0 / math.sqrt(HEAD_DIM)

        row_pos = segment * seg_rows + jnp.arange(seg_rows, dtype=jnp.int32)
        if square:
            def by_head(x):
                return x.reshape(seg_rows, heads_here, HEAD_DIM).transpose(1, 0, 2)

            chip = lax.axis_index("hi")
            core = lax.axis_index("lo")
            key_starts = [((chip ^ (b // 2)) * 2 + (core ^ (b % 2))) * seg_rows for b in range(8)]
            queries, keys, values = by_head(query_proj), by_head(key_proj), by_head(value_proj)
            split = heads_here // 2
            parts = []
            for lo_head, hi_head in ((0, split), (split, heads_here)):
                key_blocks = gather_blocks_square(keys[lo_head:hi_head])
                value_blocks = gather_blocks_square(values[lo_head:hi_head])
                parts.append(
                    attention_by_head(
                        queries[lo_head:hi_head], key_blocks, value_blocks, row_pos, key_starts
                    )
                )
            ratio = jnp.concatenate(parts, axis=0)
        else:
            both = gather_seq(jnp.concatenate([key_proj, value_proj], axis=1))
            total_rows = both.shape[0]
            keys = both[:, :feat_width].reshape(total_rows, heads_here, HEAD_DIM)
            values = both[:, feat_width:].reshape(total_rows, heads_here, HEAD_DIM)
            key_pos = jnp.arange(total_rows, dtype=jnp.int32)
            queries = query_proj.reshape(seg_rows, heads_here, HEAD_DIM)
            scores = (
                jnp.einsum("qhd,khd->hqk", queries, keys, preferred_element_type=jnp.float32)
                * score_scale
            )
            allowed = (key_pos[None, :] <= row_pos[:, None])[None]
            scores = jnp.where(allowed, scores, -1e30)
            row_max = jnp.max(scores, axis=-1)
            weights = jnp.where(allowed, jnp.exp(scores - row_max[..., None]), 0.0)
            row_total = jnp.sum(weights, axis=-1)
            numer = jnp.einsum(
                "hqk,khd->hqd", weights.astype(jnp.bfloat16), values, preferred_element_type=jnp.float32
            )
            ratio = numer / row_total[..., None]
        local_context = ratio.transpose(1, 0, 2).reshape(seg_rows, feat_width).astype(jnp.bfloat16)

        if square:
            chip = lax.axis_index("hi")
            core = lax.axis_index("lo")
            blocks = gather_blocks_square(local_context)
            width = out_weight.shape[1]
            by_row = jnp.zeros((seg_rows, seq_count * width), jnp.bfloat16)
            for b, block in enumerate(blocks):
                r, t = b // 2, b % 2
                partial = jnp.dot(block, out_weight, preferred_element_type=jnp.float32).astype(
                    jnp.bfloat16
                )
                if b:
                    pairs = [(h * 2 + l, (h ^ r) * 2 + (l ^ t)) for h in range(4) for l in range(2)]
                    partial = lax.ppermute(partial, SEQ, pairs)
                source = (chip ^ r) * 2 + (core ^ t)
                by_row = lax.dynamic_update_slice(by_row, partial, (0, source * width))
            ordered = lax.psum_scatter(by_row, "chan", scatter_dimension=1, tiled=True)
            return (residual.astype(jnp.float32) + ordered.astype(jnp.float32)).astype(jnp.bfloat16)
        gathered = gather_seq(local_context)
        group = seq_count // chan_count
        chunks = 2
        width = out_weight.shape[1] // chunks
        reduced = []
        for j in range(chunks):
            partial = jnp.dot(
                gathered, out_weight[:, j * width : (j + 1) * width], preferred_element_type=jnp.float32
            ).astype(jnp.bfloat16)
            by_row = lax.all_to_all(partial, SEQ, split_axis=0, concat_axis=1, tiled=True)
            reduced.append(
                lax.psum_scatter(by_row, "chan", scatter_dimension=1, tiled=True)
            )
        ordered = jnp.concatenate(
            [part[:, b * width : (b + 1) * width] for b in range(group) for part in reduced], axis=1
        )
        return (residual.astype(jnp.float32) + ordered.astype(jnp.float32)).astype(jnp.bfloat16)

    return per_device


def solution(mesh):
    seq_size, chan_size = mesh.devices.shape
    n_lo = cores_per_chip_along_seq(mesh)
    split = Mesh(
        mesh.devices.reshape(seq_size // n_lo, n_lo, chan_size), ("hi", "lo", mesh.axis_names[1])
    )
    rows_cols = P(SEQ, "chan")
    placed = (rows_cols, rows_cols, rows_cols, rows_cols, P("chan", SEQ))
    return jax.shard_map(
        make_per_device(is_square_of_chips(mesh, n_lo)),
        mesh=split,
        in_specs=placed,
        out_specs=rows_cols,
        check_vma=False,
    )
```

```python
import math

import jax
import jax.numpy as jnp
import numpy as np
from jax import lax
from jax.sharding import Mesh
from jax.sharding import PartitionSpec as P

HEAD_DIM = 128
SEQ = ("hi", "lo")


def cores_per_chip_along_seq(mesh):
    column = mesh.devices[:, 0]
    first = tuple(column[0].coords)
    count = 1
    while count < len(column) and tuple(column[count].coords) == first:
        count += 1
    return count


def is_square_of_chips(mesh, n_lo):
    column = mesh.devices[::n_lo, 0]
    if n_lo != 2 or len(column) != 4:
        return False
    coords = [np.array(d.coords) for d in column]
    for i in range(4):
        for flip in (1, 2):
            if np.abs(coords[i] - coords[i ^ flip]).sum() != 1:
                return False
    return True


def swap(axis, flip, n):
    return [(i, i ^ flip) for i in range(n)]


def assemble(pieces, rows, width, dtype):
    out = jnp.zeros((len(pieces) * rows, width), dtype)
    for piece, slot in pieces:
        out = lax.dynamic_update_slice(out, piece, (slot * rows, 0))
    return out


def gather_seq_square(x):
    rows, width = x.shape
    half = rows // 2
    chip = lax.axis_index("hi")
    core = lax.axis_index("lo")
    from_x = lax.ppermute(x, "hi", swap("hi", 1, 4))
    from_y = lax.ppermute(x, "hi", swap("hi", 2, 4))
    diag = jnp.concatenate(
        [
            lax.ppermute(from_y[:half], "hi", swap("hi", 1, 4)),
            lax.ppermute(from_x[half:], "hi", swap("hi", 2, 4)),
        ],
        axis=0,
    )
    mine = [(x, chip), (from_x, chip ^ 1), (from_y, chip ^ 2), (diag, chip ^ 3)]
    pieces = []
    for block, source in mine:
        pieces.append((block, source * 2 + core))
        pieces.append((lax.ppermute(block, "lo", [(0, 1), (1, 0)]), source * 2 + (1 - core)))
    return assemble(pieces, rows, width, x.dtype)


def gather_blocks_square(x):
    half = x.shape[0] // 2
    from_x = lax.ppermute(x, "hi", swap("hi", 1, 4))
    from_y = lax.ppermute(x, "hi", swap("hi", 2, 4))
    diag = jnp.concatenate(
        [
            lax.ppermute(from_y[:half], "hi", swap("hi", 1, 4)),
            lax.ppermute(from_x[half:], "hi", swap("hi", 2, 4)),
        ],
        axis=0,
    )
    blocks = []
    for block in (x, from_x, from_y, diag):
        blocks.append(block)
        blocks.append(lax.ppermute(block, "lo", [(0, 1), (1, 0)]))
    return blocks


def attention_by_head(queries, key_blocks, value_blocks, row_pos, key_starts):
    score_scale = 1.0 / math.sqrt(HEAD_DIM)
    scores = []
    masks = []
    for keys, start in zip(key_blocks, key_starts):
        part = (
            jnp.einsum("hqd,hkd->hqk", queries, keys, preferred_element_type=jnp.float32)
            * score_scale
        )
        key_pos = start + jnp.arange(keys.shape[1], dtype=jnp.int32)
        allowed = (key_pos[None, :] <= row_pos[:, None])[None]
        scores.append(jnp.where(allowed, part, -1e30))
        masks.append(allowed)
    row_max = scores[0].max(axis=-1)
    for part in scores[1:]:
        row_max = jnp.maximum(row_max, part.max(axis=-1))
    row_total = None
    numer = None
    for part, allowed, values in zip(scores, masks, value_blocks):
        weights = jnp.where(allowed, jnp.exp(part - row_max[..., None]), 0.0)
        total = jnp.sum(weights, axis=-1)
        term = jnp.einsum(
            "hqk,hkd->hqd", weights.astype(jnp.bfloat16), values, preferred_element_type=jnp.float32
        )
        row_total = total if row_total is None else row_total + total
        numer = term if numer is None else numer + term
    return numer / row_total[..., None]


def gather_same_core(x):
    half = x.shape[0] // 2
    from_x = lax.ppermute(x, "hi", swap("hi", 1, 4))
    from_y = lax.ppermute(x, "hi", swap("hi", 2, 4))
    diag = jnp.concatenate(
        [
            lax.ppermute(from_y[:half], "hi", swap("hi", 1, 4)),
            lax.ppermute(from_x[half:], "hi", swap("hi", 2, 4)),
        ],
        axis=0,
    )
    return [x, from_x, from_y, diag]


def make_per_device(square):
    def gather_seq(x):
        if square:
            return gather_seq_square(x)
        return lax.all_gather(x, SEQ, axis=0, tiled=True)

    def per_device(query_proj, key_proj, value_proj, residual, out_weight):
        seg_rows = query_proj.shape[0]
        feat_width = query_proj.shape[1]
        heads_here = feat_width // HEAD_DIM
        seq_count = lax.axis_size("hi") * lax.axis_size("lo")
        chan_count = lax.axis_size("chan")
        segment = lax.axis_index("hi") * lax.axis_size("lo") + lax.axis_index("lo")
        score_scale = 1.0 / math.sqrt(HEAD_DIM)

        row_pos = segment * seg_rows + jnp.arange(seg_rows, dtype=jnp.int32)
        if square:
            def by_head(x):
                return x.reshape(seg_rows, heads_here, HEAD_DIM).transpose(1, 0, 2)

            key_blocks = gather_blocks_square(by_head(key_proj))
            value_blocks = gather_blocks_square(by_head(value_proj))
            chip = lax.axis_index("hi")
            core = lax.axis_index("lo")
            key_starts = [
                ((chip ^ (b // 2)) * 2 + (core ^ (b % 2))) * seg_rows for b in range(len(key_blocks))
            ]
            ratio = attention_by_head(by_head(query_proj), key_blocks, value_blocks, row_pos, key_starts)
        else:
            both = gather_seq(jnp.concatenate([key_proj, value_proj], axis=1))
            total_rows = both.shape[0]
            keys = both[:, :feat_width].reshape(total_rows, heads_here, HEAD_DIM)
            values = both[:, feat_width:].reshape(total_rows, heads_here, HEAD_DIM)
            key_pos = jnp.arange(total_rows, dtype=jnp.int32)
            queries = query_proj.reshape(seg_rows, heads_here, HEAD_DIM)
            scores = (
                jnp.einsum("qhd,khd->hqk", queries, keys, preferred_element_type=jnp.float32)
                * score_scale
            )
            allowed = (key_pos[None, :] <= row_pos[:, None])[None]
            scores = jnp.where(allowed, scores, -1e30)
            row_max = jnp.max(scores, axis=-1)
            weights = jnp.where(allowed, jnp.exp(scores - row_max[..., None]), 0.0)
            row_total = jnp.sum(weights, axis=-1)
            numer = jnp.einsum(
                "hqk,khd->hqd", weights.astype(jnp.bfloat16), values, preferred_element_type=jnp.float32
            )
            ratio = numer / row_total[..., None]
        local_context = ratio.transpose(1, 0, 2).reshape(seg_rows, feat_width).astype(jnp.bfloat16)

        if square:
            chip = lax.axis_index("hi")
            core = lax.axis_index("lo")
            width = out_weight.shape[1]
            chip_weight = jnp.concatenate(
                [out_weight, lax.ppermute(out_weight, "lo", [(0, 1), (1, 0)])], axis=1
            )
            blocks = gather_same_core(local_context)
            by_row = jnp.zeros((seg_rows, seq_count * width), jnp.bfloat16)
            for r, block in enumerate(blocks):
                partial = jnp.dot(block, chip_weight, preferred_element_type=jnp.float32).astype(
                    jnp.bfloat16
                )
                if r:
                    partial = lax.ppermute(partial, "hi", swap("hi", r, 4))
                mine = (chip ^ r) * 2 + core
                other = (chip ^ r) * 2 + (1 - core)
                by_row = lax.dynamic_update_slice(by_row, partial[:, :width], (0, mine * width))
                by_row = lax.dynamic_update_slice(by_row, partial[:, width:], (0, other * width))
            ordered = lax.psum_scatter(by_row, "chan", scatter_dimension=1, tiled=True)
            return (residual.astype(jnp.float32) + ordered.astype(jnp.float32)).astype(jnp.bfloat16)
        gathered = gather_seq(local_context)
        group = seq_count // chan_count
        chunks = 2
        width = out_weight.shape[1] // chunks
        reduced = []
        for j in range(chunks):
            partial = jnp.dot(
                gathered, out_weight[:, j * width : (j + 1) * width], preferred_element_type=jnp.float32
            ).astype(jnp.bfloat16)
            by_row = lax.all_to_all(partial, SEQ, split_axis=0, concat_axis=1, tiled=True)
            reduced.append(
                lax.psum_scatter(by_row, "chan", scatter_dimension=1, tiled=True)
            )
        ordered = jnp.concatenate(
            [part[:, b * width : (b + 1) * width] for b in range(group) for part in reduced], axis=1
        )
        return (residual.astype(jnp.float32) + ordered.astype(jnp.float32)).astype(jnp.bfloat16)

    return per_device


def solution(mesh):
    seq_size, chan_size = mesh.devices.shape
    n_lo = cores_per_chip_along_seq(mesh)
    split = Mesh(
        mesh.devices.reshape(seq_size // n_lo, n_lo, chan_size), ("hi", "lo", mesh.axis_names[1])
    )
    rows_cols = P(SEQ, "chan")
    placed = (rows_cols, rows_cols, rows_cols, rows_cols, P("chan", SEQ))
    return jax.shard_map(
        make_per_device(is_square_of_chips(mesh, n_lo)),
        mesh=split,
        in_specs=placed,
        out_specs=rows_cols,
        check_vma=False,
    )
```

```python
import math

import jax
import jax.numpy as jnp
import numpy as np
from jax import lax
from jax.sharding import Mesh
from jax.sharding import PartitionSpec as P

HEAD_DIM = 128
SEQ = ("hi", "lo")


def cores_per_chip_along_seq(mesh):
    column = mesh.devices[:, 0]
    first = tuple(column[0].coords)
    count = 1
    while count < len(column) and tuple(column[count].coords) == first:
        count += 1
    return count


def is_square_of_chips(mesh, n_lo):
    column = mesh.devices[::n_lo, 0]
    if n_lo != 2 or len(column) != 4:
        return False
    coords = [np.array(d.coords) for d in column]
    for i in range(4):
        for flip in (1, 2):
            if np.abs(coords[i] - coords[i ^ flip]).sum() != 1:
                return False
    return True


def swap(axis, flip, n):
    return [(i, i ^ flip) for i in range(n)]


def assemble(pieces, rows, width, dtype):
    out = jnp.zeros((len(pieces) * rows, width), dtype)
    for piece, slot in pieces:
        out = lax.dynamic_update_slice(out, piece, (slot * rows, 0))
    return out


def gather_seq_square(x):
    rows, width = x.shape
    half = rows // 2
    chip = lax.axis_index("hi")
    core = lax.axis_index("lo")
    from_x = lax.ppermute(x, "hi", swap("hi", 1, 4))
    from_y = lax.ppermute(x, "hi", swap("hi", 2, 4))
    diag = jnp.concatenate(
        [
            lax.ppermute(from_y[:half], "hi", swap("hi", 1, 4)),
            lax.ppermute(from_x[half:], "hi", swap("hi", 2, 4)),
        ],
        axis=0,
    )
    mine = [(x, chip), (from_x, chip ^ 1), (from_y, chip ^ 2), (diag, chip ^ 3)]
    pieces = []
    for block, source in mine:
        pieces.append((block, source * 2 + core))
        pieces.append((lax.ppermute(block, "lo", [(0, 1), (1, 0)]), source * 2 + (1 - core)))
    return assemble(pieces, rows, width, x.dtype)


def gather_blocks_square(x):
    half = x.shape[0] // 2
    from_x = lax.ppermute(x, "hi", swap("hi", 1, 4))
    from_y = lax.ppermute(x, "hi", swap("hi", 2, 4))
    diag = jnp.concatenate(
        [
            lax.ppermute(from_y[:half], "hi", swap("hi", 1, 4)),
            lax.ppermute(from_x[half:], "hi", swap("hi", 2, 4)),
        ],
        axis=0,
    )
    blocks = []
    for block in (x, from_x, from_y, diag):
        blocks.append(block)
        blocks.append(lax.ppermute(block, "lo", [(0, 1), (1, 0)]))
    return blocks


def attention_by_head(queries, key_blocks, value_blocks, row_pos, key_starts):
    score_scale = 1.0 / math.sqrt(HEAD_DIM)
    scores = []
    masks = []
    for keys, start in zip(key_blocks, key_starts):
        part = (
            jnp.einsum("hqd,hkd->hqk", queries, keys, preferred_element_type=jnp.float32)
            * score_scale
        )
        key_pos = start + jnp.arange(keys.shape[1], dtype=jnp.int32)
        allowed = (key_pos[None, :] <= row_pos[:, None])[None]
        scores.append(jnp.where(allowed, part, -1e30))
        masks.append(allowed)
    row_max = scores[0].max(axis=-1)
    for part in scores[1:]:
        row_max = jnp.maximum(row_max, part.max(axis=-1))
    row_total = None
    numer = None
    for part, allowed, values in zip(scores, masks, value_blocks):
        weights = jnp.where(allowed, jnp.exp(part - row_max[..., None]), 0.0)
        total = jnp.sum(weights, axis=-1)
        term = jnp.einsum(
            "hqk,hkd->hqd", weights.astype(jnp.bfloat16), values, preferred_element_type=jnp.float32
        )
        row_total = total if row_total is None else row_total + total
        numer = term if numer is None else numer + term
    return numer / row_total[..., None]


def gather_same_core(x):
    half = x.shape[0] // 2
    from_x = lax.ppermute(x, "hi", swap("hi", 1, 4))
    from_y = lax.ppermute(x, "hi", swap("hi", 2, 4))
    diag = jnp.concatenate(
        [
            lax.ppermute(from_y[:half], "hi", swap("hi", 1, 4)),
            lax.ppermute(from_x[half:], "hi", swap("hi", 2, 4)),
        ],
        axis=0,
    )
    return [x, from_x, from_y, diag]


def make_per_device(square):
    def gather_seq(x):
        if square:
            return gather_seq_square(x)
        return lax.all_gather(x, SEQ, axis=0, tiled=True)

    def per_device(query_proj, key_proj, value_proj, residual, out_weight):
        seg_rows = query_proj.shape[0]
        feat_width = query_proj.shape[1]
        heads_here = feat_width // HEAD_DIM
        seq_count = lax.axis_size("hi") * lax.axis_size("lo")
        chan_count = lax.axis_size("chan")
        segment = lax.axis_index("hi") * lax.axis_size("lo") + lax.axis_index("lo")
        score_scale = 1.0 / math.sqrt(HEAD_DIM)

        row_pos = segment * seg_rows + jnp.arange(seg_rows, dtype=jnp.int32)
        if square:
            def by_head(x):
                return x.reshape(seg_rows, heads_here, HEAD_DIM).transpose(1, 0, 2)

            key_blocks = gather_blocks_square(by_head(key_proj))
            value_blocks = gather_blocks_square(by_head(value_proj))
            chip = lax.axis_index("hi")
            core = lax.axis_index("lo")
            key_starts = [
                ((chip ^ (b // 2)) * 2 + (core ^ (b % 2))) * seg_rows for b in range(len(key_blocks))
            ]
            ratio = attention_by_head(by_head(query_proj), key_blocks, value_blocks, row_pos, key_starts)
        else:
            both = gather_seq(jnp.concatenate([key_proj, value_proj], axis=1))
            total_rows = both.shape[0]
            keys = both[:, :feat_width].reshape(total_rows, heads_here, HEAD_DIM)
            values = both[:, feat_width:].reshape(total_rows, heads_here, HEAD_DIM)
            key_pos = jnp.arange(total_rows, dtype=jnp.int32)
            queries = query_proj.reshape(seg_rows, heads_here, HEAD_DIM)
            scores = (
                jnp.einsum("qhd,khd->hqk", queries, keys, preferred_element_type=jnp.float32)
                * score_scale
            )
            allowed = (key_pos[None, :] <= row_pos[:, None])[None]
            scores = jnp.where(allowed, scores, -1e30)
            row_max = jnp.max(scores, axis=-1)
            weights = jnp.where(allowed, jnp.exp(scores - row_max[..., None]), 0.0)
            row_total = jnp.sum(weights, axis=-1)
            numer = jnp.einsum(
                "hqk,khd->hqd", weights.astype(jnp.bfloat16), values, preferred_element_type=jnp.float32
            )
            ratio = numer / row_total[..., None]
        local_context = ratio.transpose(1, 0, 2).reshape(seg_rows, feat_width).astype(jnp.bfloat16)

        if square:
            chip = lax.axis_index("hi")
            core = lax.axis_index("lo")
            width = out_weight.shape[1]
            chip_weight = jnp.concatenate(
                [out_weight, lax.ppermute(out_weight, "lo", [(0, 1), (1, 0)])], axis=1
            )
            blocks = gather_same_core(local_context)
            by_row = jnp.zeros((seg_rows, seq_count * width), jnp.bfloat16)
            for r, block in enumerate(blocks):
                partial = jnp.dot(block, chip_weight, preferred_element_type=jnp.float32).astype(
                    jnp.bfloat16
                )
                if r == 3:
                    half = partial.shape[0] // 2
                    first = lax.ppermute(
                        lax.ppermute(partial[:half], "hi", swap("hi", 1, 4)), "hi", swap("hi", 2, 4)
                    )
                    second = lax.ppermute(
                        lax.ppermute(partial[half:], "hi", swap("hi", 2, 4)), "hi", swap("hi", 1, 4)
                    )
                    partial = jnp.concatenate([first, second], axis=0)
                elif r:
                    partial = lax.ppermute(partial, "hi", swap("hi", r, 4))
                mine = (chip ^ r) * 2 + core
                other = (chip ^ r) * 2 + (1 - core)
                by_row = lax.dynamic_update_slice(by_row, partial[:, :width], (0, mine * width))
                by_row = lax.dynamic_update_slice(by_row, partial[:, width:], (0, other * width))
            ordered = lax.psum_scatter(by_row, "chan", scatter_dimension=1, tiled=True)
            return (residual.astype(jnp.float32) + ordered.astype(jnp.float32)).astype(jnp.bfloat16)
        gathered = gather_seq(local_context)
        group = seq_count // chan_count
        chunks = 2
        width = out_weight.shape[1] // chunks
        reduced = []
        for j in range(chunks):
            partial = jnp.dot(
                gathered, out_weight[:, j * width : (j + 1) * width], preferred_element_type=jnp.float32
            ).astype(jnp.bfloat16)
            by_row = lax.all_to_all(partial, SEQ, split_axis=0, concat_axis=1, tiled=True)
            reduced.append(
                lax.psum_scatter(by_row, "chan", scatter_dimension=1, tiled=True)
            )
        ordered = jnp.concatenate(
            [part[:, b * width : (b + 1) * width] for b in range(group) for part in reduced], axis=1
        )
        return (residual.astype(jnp.float32) + ordered.astype(jnp.float32)).astype(jnp.bfloat16)

    return per_device


def solution(mesh):
    seq_size, chan_size = mesh.devices.shape
    n_lo = cores_per_chip_along_seq(mesh)
    split = Mesh(
        mesh.devices.reshape(seq_size // n_lo, n_lo, chan_size), ("hi", "lo", mesh.axis_names[1])
    )
    rows_cols = P(SEQ, "chan")
    placed = (rows_cols, rows_cols, rows_cols, rows_cols, P("chan", SEQ))
    return jax.shard_map(
        make_per_device(is_square_of_chips(mesh, n_lo)),
        mesh=split,
        in_specs=placed,
        out_specs=rows_cols,
        check_vma=False,
    )
```

```python
import math

import jax
import jax.numpy as jnp
import numpy as np
from jax import lax
from jax.sharding import Mesh
from jax.sharding import PartitionSpec as P

HEAD_DIM = 128
SEQ = ("hi", "lo")


def cores_per_chip_along_seq(mesh):
    column = mesh.devices[:, 0]
    first = tuple(column[0].coords)
    count = 1
    while count < len(column) and tuple(column[count].coords) == first:
        count += 1
    return count


def is_square_of_chips(mesh, n_lo):
    column = mesh.devices[::n_lo, 0]
    if n_lo != 2 or len(column) != 4:
        return False
    coords = [np.array(d.coords) for d in column]
    for i in range(4):
        for flip in (1, 2):
            if np.abs(coords[i] - coords[i ^ flip]).sum() != 1:
                return False
    return True


def swap(axis, flip, n):
    return [(i, i ^ flip) for i in range(n)]


def assemble(pieces, rows, width, dtype):
    out = jnp.zeros((len(pieces) * rows, width), dtype)
    for piece, slot in pieces:
        out = lax.dynamic_update_slice(out, piece, (slot * rows, 0))
    return out


def gather_seq_square(x):
    rows, width = x.shape
    half = rows // 2
    chip = lax.axis_index("hi")
    core = lax.axis_index("lo")
    from_x = lax.ppermute(x, "hi", swap("hi", 1, 4))
    from_y = lax.ppermute(x, "hi", swap("hi", 2, 4))
    diag = jnp.concatenate(
        [
            lax.ppermute(from_y[:half], "hi", swap("hi", 1, 4)),
            lax.ppermute(from_x[half:], "hi", swap("hi", 2, 4)),
        ],
        axis=0,
    )
    mine = [(x, chip), (from_x, chip ^ 1), (from_y, chip ^ 2), (diag, chip ^ 3)]
    pieces = []
    for block, source in mine:
        pieces.append((block, source * 2 + core))
        pieces.append((lax.ppermute(block, "lo", [(0, 1), (1, 0)]), source * 2 + (1 - core)))
    return assemble(pieces, rows, width, x.dtype)


def gather_blocks_square(x):
    half = x.shape[0] // 2
    from_x = lax.ppermute(x, "hi", swap("hi", 1, 4))
    from_y = lax.ppermute(x, "hi", swap("hi", 2, 4))
    diag = jnp.concatenate(
        [
            lax.ppermute(from_y[:half], "hi", swap("hi", 1, 4)),
            lax.ppermute(from_x[half:], "hi", swap("hi", 2, 4)),
        ],
        axis=0,
    )
    blocks = []
    for block in (x, from_x, from_y, diag):
        blocks.append(block)
        blocks.append(lax.ppermute(block, "lo", [(0, 1), (1, 0)]))
    return blocks


def attention_by_head(queries, key_blocks, value_blocks, row_pos, key_starts):
    score_scale = 1.0 / math.sqrt(HEAD_DIM)
    scores = []
    masks = []
    for keys, start in zip(key_blocks, key_starts):
        part = (
            jnp.einsum("hqd,hkd->hqk", queries, keys, preferred_element_type=jnp.float32)
            * score_scale
        )
        key_pos = start + jnp.arange(keys.shape[1], dtype=jnp.int32)
        allowed = (key_pos[None, :] <= row_pos[:, None])[None]
        scores.append(jnp.where(allowed, part, -1e30))
        masks.append(allowed)
    row_max = scores[0].max(axis=-1)
    for part in scores[1:]:
        row_max = jnp.maximum(row_max, part.max(axis=-1))
    row_total = None
    numer = None
    for part, allowed, values in zip(scores, masks, value_blocks):
        weights = jnp.where(allowed, jnp.exp(part - row_max[..., None]), 0.0)
        total = jnp.sum(weights, axis=-1)
        term = jnp.einsum(
            "hqk,hkd->hqd", weights.astype(jnp.bfloat16), values, preferred_element_type=jnp.float32
        )
        row_total = total if row_total is None else row_total + total
        numer = term if numer is None else numer + term
    return numer / row_total[..., None]


def make_per_device(square):
    def gather_seq(x):
        if square:
            return gather_seq_square(x)
        return lax.all_gather(x, SEQ, axis=0, tiled=True)

    def per_device(query_proj, key_proj, value_proj, residual, out_weight):
        seg_rows = query_proj.shape[0]
        feat_width = query_proj.shape[1]
        heads_here = feat_width // HEAD_DIM
        seq_count = lax.axis_size("hi") * lax.axis_size("lo")
        chan_count = lax.axis_size("chan")
        segment = lax.axis_index("hi") * lax.axis_size("lo") + lax.axis_index("lo")
        score_scale = 1.0 / math.sqrt(HEAD_DIM)

        row_pos = segment * seg_rows + jnp.arange(seg_rows, dtype=jnp.int32)
        if square:
            def by_head(x):
                return x.reshape(seg_rows, heads_here, HEAD_DIM).transpose(1, 0, 2)

            key_blocks = gather_blocks_square(by_head(key_proj))
            value_blocks = gather_blocks_square(by_head(value_proj))
            chip = lax.axis_index("hi")
            core = lax.axis_index("lo")
            key_starts = [
                ((chip ^ (b // 2)) * 2 + (core ^ (b % 2))) * seg_rows for b in range(len(key_blocks))
            ]
            ratio = attention_by_head(by_head(query_proj), key_blocks, value_blocks, row_pos, key_starts)
        else:
            both = gather_seq(jnp.concatenate([key_proj, value_proj], axis=1))
            total_rows = both.shape[0]
            keys = both[:, :feat_width].reshape(total_rows, heads_here, HEAD_DIM)
            values = both[:, feat_width:].reshape(total_rows, heads_here, HEAD_DIM)
            key_pos = jnp.arange(total_rows, dtype=jnp.int32)
            queries = query_proj.reshape(seg_rows, heads_here, HEAD_DIM)
            scores = (
                jnp.einsum("qhd,khd->hqk", queries, keys, preferred_element_type=jnp.float32)
                * score_scale
            )
            allowed = (key_pos[None, :] <= row_pos[:, None])[None]
            scores = jnp.where(allowed, scores, -1e30)
            row_max = jnp.max(scores, axis=-1)
            weights = jnp.where(allowed, jnp.exp(scores - row_max[..., None]), 0.0)
            row_total = jnp.sum(weights, axis=-1)
            numer = jnp.einsum(
                "hqk,khd->hqd", weights.astype(jnp.bfloat16), values, preferred_element_type=jnp.float32
            )
            ratio = numer / row_total[..., None]
        local_context = ratio.transpose(1, 0, 2).reshape(seg_rows, feat_width).astype(jnp.bfloat16)

        if square:
            chip = lax.axis_index("hi")
            core = lax.axis_index("lo")
            blocks = gather_blocks_square(local_context)
            width = out_weight.shape[1]
            by_row = jnp.zeros((chan_count, seg_rows, 2 * width), jnp.bfloat16)
            for b, block in enumerate(blocks):
                r, t = b // 2, b % 2
                partial = jnp.dot(block, out_weight, preferred_element_type=jnp.float32).astype(
                    jnp.bfloat16
                )
                if b:
                    pairs = [(h * 2 + l, (h ^ r) * 2 + (l ^ t)) for h in range(4) for l in range(2)]
                    partial = lax.ppermute(partial, SEQ, pairs)
                source = (chip ^ r) * 2 + (core ^ t)
                by_row = lax.dynamic_update_slice(
                    by_row, partial[None], (source // 2, 0, (source % 2) * width)
                )
            ordered = lax.psum_scatter(by_row, "chan", scatter_dimension=0, tiled=True)[0]
            return (residual.astype(jnp.float32) + ordered.astype(jnp.float32)).astype(jnp.bfloat16)
        gathered = gather_seq(local_context)
        group = seq_count // chan_count
        chunks = 2
        width = out_weight.shape[1] // chunks
        reduced = []
        for j in range(chunks):
            partial = jnp.dot(
                gathered, out_weight[:, j * width : (j + 1) * width], preferred_element_type=jnp.float32
            ).astype(jnp.bfloat16)
            by_row = lax.all_to_all(partial, SEQ, split_axis=0, concat_axis=1, tiled=True)
            reduced.append(
                lax.psum_scatter(by_row, "chan", scatter_dimension=1, tiled=True)
            )
        ordered = jnp.concatenate(
            [part[:, b * width : (b + 1) * width] for b in range(group) for part in reduced], axis=1
        )
        return (residual.astype(jnp.float32) + ordered.astype(jnp.float32)).astype(jnp.bfloat16)

    return per_device


def solution(mesh):
    seq_size, chan_size = mesh.devices.shape
    n_lo = cores_per_chip_along_seq(mesh)
    split = Mesh(
        mesh.devices.reshape(seq_size // n_lo, n_lo, chan_size), ("hi", "lo", mesh.axis_names[1])
    )
    rows_cols = P(SEQ, "chan")
    placed = (rows_cols, rows_cols, rows_cols, rows_cols, P("chan", SEQ))
    return jax.shard_map(
        make_per_device(is_square_of_chips(mesh, n_lo)),
        mesh=split,
        in_specs=placed,
        out_specs=rows_cols,
        check_vma=False,
    )
```

```python
import math

import jax
import jax.numpy as jnp
import numpy as np
from jax import lax
from jax.sharding import Mesh
from jax.sharding import PartitionSpec as P

HEAD_DIM = 128
SEQ = ("hi", "lo")


def cores_per_chip_along_seq(mesh):
    column = mesh.devices[:, 0]
    first = tuple(column[0].coords)
    count = 1
    while count < len(column) and tuple(column[count].coords) == first:
        count += 1
    return count


def is_square_of_chips(mesh, n_lo):
    column = mesh.devices[::n_lo, 0]
    if n_lo != 2 or len(column) != 4:
        return False
    coords = [np.array(d.coords) for d in column]
    for i in range(4):
        for flip in (1, 2):
            if np.abs(coords[i] - coords[i ^ flip]).sum() != 1:
                return False
    return True


def swap(axis, flip, n):
    return [(i, i ^ flip) for i in range(n)]


def assemble(pieces, rows, width, dtype):
    out = jnp.zeros((len(pieces) * rows, width), dtype)
    for piece, slot in pieces:
        out = lax.dynamic_update_slice(out, piece, (slot * rows, 0))
    return out


def gather_seq_square(x):
    rows, width = x.shape
    half = rows // 2
    chip = lax.axis_index("hi")
    core = lax.axis_index("lo")
    from_x = lax.ppermute(x, "hi", swap("hi", 1, 4))
    from_y = lax.ppermute(x, "hi", swap("hi", 2, 4))
    diag = jnp.concatenate(
        [
            lax.ppermute(from_y[:half], "hi", swap("hi", 1, 4)),
            lax.ppermute(from_x[half:], "hi", swap("hi", 2, 4)),
        ],
        axis=0,
    )
    mine = [(x, chip), (from_x, chip ^ 1), (from_y, chip ^ 2), (diag, chip ^ 3)]
    pieces = []
    for block, source in mine:
        pieces.append((block, source * 2 + core))
        pieces.append((lax.ppermute(block, "lo", [(0, 1), (1, 0)]), source * 2 + (1 - core)))
    return assemble(pieces, rows, width, x.dtype)


def gather_blocks_square(x):
    half = x.shape[0] // 2
    from_x = lax.ppermute(x, "hi", swap("hi", 1, 4))
    from_y = lax.ppermute(x, "hi", swap("hi", 2, 4))
    diag = jnp.concatenate(
        [
            lax.ppermute(from_y[:half], "hi", swap("hi", 1, 4)),
            lax.ppermute(from_x[half:], "hi", swap("hi", 2, 4)),
        ],
        axis=0,
    )
    blocks = []
    for block in (x, from_x, from_y, diag):
        blocks.append(block)
        blocks.append(lax.ppermute(block, "lo", [(0, 1), (1, 0)]))
    return blocks


def attention_by_head(queries, key_blocks, value_blocks, row_pos, key_starts):
    score_scale = 1.0 / math.sqrt(HEAD_DIM)
    scores = []
    masks = []
    for keys, start in zip(key_blocks, key_starts):
        part = (
            jnp.einsum("hqd,hkd->hqk", queries, keys, preferred_element_type=jnp.float32)
            * score_scale
        )
        key_pos = start + jnp.arange(keys.shape[1], dtype=jnp.int32)
        allowed = (key_pos[None, :] <= row_pos[:, None])[None]
        scores.append(jnp.where(allowed, part, -1e30))
        masks.append(allowed)
    row_max = scores[0].max(axis=-1)
    for part in scores[1:]:
        row_max = jnp.maximum(row_max, part.max(axis=-1))
    row_total = None
    numer = None
    for part, allowed, values in zip(scores, masks, value_blocks):
        weights = jnp.where(allowed, jnp.exp(part - row_max[..., None]), 0.0)
        total = jnp.sum(weights, axis=-1)
        term = jnp.einsum(
            "hqk,hkd->hqd", weights.astype(jnp.bfloat16), values, preferred_element_type=jnp.float32
        )
        row_total = total if row_total is None else row_total + total
        numer = term if numer is None else numer + term
    return numer / row_total[..., None]


def make_per_device(square):
    def gather_seq(x):
        if square:
            return gather_seq_square(x)
        return lax.all_gather(x, SEQ, axis=0, tiled=True)

    def per_device(query_proj, key_proj, value_proj, residual, out_weight):
        seg_rows = query_proj.shape[0]
        feat_width = query_proj.shape[1]
        heads_here = feat_width // HEAD_DIM
        seq_count = lax.axis_size("hi") * lax.axis_size("lo")
        chan_count = lax.axis_size("chan")
        segment = lax.axis_index("hi") * lax.axis_size("lo") + lax.axis_index("lo")
        score_scale = 1.0 / math.sqrt(HEAD_DIM)

        row_pos = segment * seg_rows + jnp.arange(seg_rows, dtype=jnp.int32)
        if square:
            def by_head(x):
                return x.reshape(seg_rows, heads_here, HEAD_DIM).transpose(1, 0, 2)

            key_blocks = gather_blocks_square(by_head(key_proj))
            value_blocks = gather_blocks_square(by_head(value_proj))
            chip = lax.axis_index("hi")
            core = lax.axis_index("lo")
            key_starts = [
                ((chip ^ (b // 2)) * 2 + (core ^ (b % 2))) * seg_rows for b in range(len(key_blocks))
            ]
            ratio = attention_by_head(by_head(query_proj), key_blocks, value_blocks, row_pos, key_starts)
        else:
            both = gather_seq(jnp.concatenate([key_proj, value_proj], axis=1))
            total_rows = both.shape[0]
            keys = both[:, :feat_width].reshape(total_rows, heads_here, HEAD_DIM)
            values = both[:, feat_width:].reshape(total_rows, heads_here, HEAD_DIM)
            key_pos = jnp.arange(total_rows, dtype=jnp.int32)
            queries = query_proj.reshape(seg_rows, heads_here, HEAD_DIM)
            scores = (
                jnp.einsum("qhd,khd->hqk", queries, keys, preferred_element_type=jnp.float32)
                * score_scale
            )
            allowed = (key_pos[None, :] <= row_pos[:, None])[None]
            scores = jnp.where(allowed, scores, -1e30)
            row_max = jnp.max(scores, axis=-1)
            weights = jnp.where(allowed, jnp.exp(scores - row_max[..., None]), 0.0)
            row_total = jnp.sum(weights, axis=-1)
            numer = jnp.einsum(
                "hqk,khd->hqd", weights.astype(jnp.bfloat16), values, preferred_element_type=jnp.float32
            )
            ratio = numer / row_total[..., None]
        local_context = ratio.transpose(1, 0, 2).reshape(seg_rows, feat_width).astype(jnp.bfloat16)

        if square:
            chip = lax.axis_index("hi")
            core = lax.axis_index("lo")
            blocks = gather_blocks_square(local_context)
            width = out_weight.shape[1]
            by_row = jnp.zeros((chan_count, seg_rows, 2 * width), jnp.bfloat16)
            for b, block in enumerate(blocks):
                r, t = b // 2, b % 2
                partial = jnp.dot(block, out_weight, preferred_element_type=jnp.float32).astype(
                    jnp.bfloat16
                )
                if r == 3:
                    first, second = (1, 2) if t == 0 else (2, 1)
                    partial = lax.ppermute(partial, "hi", swap("hi", first, 4))
                    pairs = [(h * 2 + l, (h ^ second) * 2 + (l ^ t)) for h in range(4) for l in range(2)]
                    partial = lax.ppermute(partial, SEQ, pairs)
                elif b:
                    pairs = [(h * 2 + l, (h ^ r) * 2 + (l ^ t)) for h in range(4) for l in range(2)]
                    partial = lax.ppermute(partial, SEQ, pairs)
                source = (chip ^ r) * 2 + (core ^ t)
                by_row = lax.dynamic_update_slice(
                    by_row, partial[None], (source // 2, 0, (source % 2) * width)
                )
            ordered = lax.psum_scatter(by_row, "chan", scatter_dimension=0, tiled=True)[0]
            return (residual.astype(jnp.float32) + ordered.astype(jnp.float32)).astype(jnp.bfloat16)
        gathered = gather_seq(local_context)
        group = seq_count // chan_count
        chunks = 2
        width = out_weight.shape[1] // chunks
        reduced = []
        for j in range(chunks):
            partial = jnp.dot(
                gathered, out_weight[:, j * width : (j + 1) * width], preferred_element_type=jnp.float32
            ).astype(jnp.bfloat16)
            by_row = lax.all_to_all(partial, SEQ, split_axis=0, concat_axis=1, tiled=True)
            reduced.append(
                lax.psum_scatter(by_row, "chan", scatter_dimension=1, tiled=True)
            )
        ordered = jnp.concatenate(
            [part[:, b * width : (b + 1) * width] for b in range(group) for part in reduced], axis=1
        )
        return (residual.astype(jnp.float32) + ordered.astype(jnp.float32)).astype(jnp.bfloat16)

    return per_device


def solution(mesh):
    seq_size, chan_size = mesh.devices.shape
    n_lo = cores_per_chip_along_seq(mesh)
    split = Mesh(
        mesh.devices.reshape(seq_size // n_lo, n_lo, chan_size), ("hi", "lo", mesh.axis_names[1])
    )
    rows_cols = P(SEQ, "chan")
    placed = (rows_cols, rows_cols, rows_cols, rows_cols, P("chan", SEQ))
    return jax.shard_map(
        make_per_device(is_square_of_chips(mesh, n_lo)),
        mesh=split,
        in_specs=placed,
        out_specs=rows_cols,
        check_vma=False,
    )
```

```python
import math

import jax
import jax.numpy as jnp
import numpy as np
from jax import lax
from jax.sharding import Mesh
from jax.sharding import PartitionSpec as P

HEAD_DIM = 128
SEQ = ("hi", "lo")


def cores_per_chip_along_seq(mesh):
    column = mesh.devices[:, 0]
    first = tuple(column[0].coords)
    count = 1
    while count < len(column) and tuple(column[count].coords) == first:
        count += 1
    return count


def is_square_of_chips(mesh, n_lo):
    column = mesh.devices[::n_lo, 0]
    if n_lo != 2 or len(column) != 4:
        return False
    coords = [np.array(d.coords) for d in column]
    for i in range(4):
        for flip in (1, 2):
            if np.abs(coords[i] - coords[i ^ flip]).sum() != 1:
                return False
    return True


def swap(axis, flip, n):
    return [(i, i ^ flip) for i in range(n)]


def assemble(pieces, rows, width, dtype):
    out = jnp.zeros((len(pieces) * rows, width), dtype)
    for piece, slot in pieces:
        out = lax.dynamic_update_slice(out, piece, (slot * rows, 0))
    return out


def gather_seq_square(x):
    rows, width = x.shape
    half = rows // 2
    chip = lax.axis_index("hi")
    core = lax.axis_index("lo")
    from_x = lax.ppermute(x, "hi", swap("hi", 1, 4))
    from_y = lax.ppermute(x, "hi", swap("hi", 2, 4))
    diag = jnp.concatenate(
        [
            lax.ppermute(from_y[:half], "hi", swap("hi", 1, 4)),
            lax.ppermute(from_x[half:], "hi", swap("hi", 2, 4)),
        ],
        axis=0,
    )
    mine = [(x, chip), (from_x, chip ^ 1), (from_y, chip ^ 2), (diag, chip ^ 3)]
    pieces = []
    for block, source in mine:
        pieces.append((block, source * 2 + core))
        pieces.append((lax.ppermute(block, "lo", [(0, 1), (1, 0)]), source * 2 + (1 - core)))
    return assemble(pieces, rows, width, x.dtype)


def gather_blocks_square(x):
    half = x.shape[0] // 2
    from_x = lax.ppermute(x, "hi", swap("hi", 1, 4))
    from_y = lax.ppermute(x, "hi", swap("hi", 2, 4))
    diag = jnp.concatenate(
        [
            lax.ppermute(from_y[:half], "hi", swap("hi", 1, 4)),
            lax.ppermute(from_x[half:], "hi", swap("hi", 2, 4)),
        ],
        axis=0,
    )
    blocks = []
    for block in (x, from_x, from_y, diag):
        blocks.append(block)
        blocks.append(lax.ppermute(block, "lo", [(0, 1), (1, 0)]))
    return blocks


def attention_by_head(queries, key_blocks, value_blocks, row_pos, key_starts):
    score_scale = 1.0 / math.sqrt(HEAD_DIM)
    scores = []
    masks = []
    for keys, start in zip(key_blocks, key_starts):
        part = (
            jnp.einsum("hqd,hkd->hqk", queries, keys, preferred_element_type=jnp.float32)
            * score_scale
        )
        key_pos = start + jnp.arange(keys.shape[1], dtype=jnp.int32)
        allowed = (key_pos[None, :] <= row_pos[:, None])[None]
        scores.append(jnp.where(allowed, part, -1e30))
        masks.append(allowed)
    row_max = scores[0].max(axis=-1)
    for part in scores[1:]:
        row_max = jnp.maximum(row_max, part.max(axis=-1))
    row_total = None
    numer = None
    for part, allowed, values in zip(scores, masks, value_blocks):
        weights = jnp.where(allowed, jnp.exp(part - row_max[..., None]), 0.0)
        total = jnp.sum(weights, axis=-1)
        term = jnp.einsum(
            "hqk,hkd->hqd", weights.astype(jnp.bfloat16), values, preferred_element_type=jnp.float32
        )
        row_total = total if row_total is None else row_total + total
        numer = term if numer is None else numer + term
    return numer / row_total[..., None]


def make_per_device(square):
    def gather_seq(x):
        if square:
            return gather_seq_square(x)
        return lax.all_gather(x, SEQ, axis=0, tiled=True)

    def per_device(query_proj, key_proj, value_proj, residual, out_weight):
        seg_rows = query_proj.shape[0]
        feat_width = query_proj.shape[1]
        heads_here = feat_width // HEAD_DIM
        seq_count = lax.axis_size("hi") * lax.axis_size("lo")
        chan_count = lax.axis_size("chan")
        segment = lax.axis_index("hi") * lax.axis_size("lo") + lax.axis_index("lo")
        score_scale = 1.0 / math.sqrt(HEAD_DIM)

        row_pos = segment * seg_rows + jnp.arange(seg_rows, dtype=jnp.int32)
        if square:
            def by_head(x):
                return x.reshape(seg_rows, heads_here, HEAD_DIM).transpose(1, 0, 2)

            key_blocks = gather_blocks_square(by_head(key_proj))
            value_blocks = gather_blocks_square(by_head(value_proj))
            chip = lax.axis_index("hi")
            core = lax.axis_index("lo")
            key_starts = [
                ((chip ^ (b // 2)) * 2 + (core ^ (b % 2))) * seg_rows for b in range(len(key_blocks))
            ]
            query_after, _ = lax.optimization_barrier((query_proj, key_blocks[2]))
            ratio = attention_by_head(by_head(query_after), key_blocks, value_blocks, row_pos, key_starts)
        else:
            both = gather_seq(jnp.concatenate([key_proj, value_proj], axis=1))
            total_rows = both.shape[0]
            keys = both[:, :feat_width].reshape(total_rows, heads_here, HEAD_DIM)
            values = both[:, feat_width:].reshape(total_rows, heads_here, HEAD_DIM)
            key_pos = jnp.arange(total_rows, dtype=jnp.int32)
            queries = query_proj.reshape(seg_rows, heads_here, HEAD_DIM)
            scores = (
                jnp.einsum("qhd,khd->hqk", queries, keys, preferred_element_type=jnp.float32)
                * score_scale
            )
            allowed = (key_pos[None, :] <= row_pos[:, None])[None]
            scores = jnp.where(allowed, scores, -1e30)
            row_max = jnp.max(scores, axis=-1)
            weights = jnp.where(allowed, jnp.exp(scores - row_max[..., None]), 0.0)
            row_total = jnp.sum(weights, axis=-1)
            numer = jnp.einsum(
                "hqk,khd->hqd", weights.astype(jnp.bfloat16), values, preferred_element_type=jnp.float32
            )
            ratio = numer / row_total[..., None]
        local_context = ratio.transpose(1, 0, 2).reshape(seg_rows, feat_width).astype(jnp.bfloat16)

        if square:
            chip = lax.axis_index("hi")
            core = lax.axis_index("lo")
            blocks = gather_blocks_square(local_context)
            width = out_weight.shape[1]
            by_row = jnp.zeros((chan_count, seg_rows, 2 * width), jnp.bfloat16)
            for b, block in enumerate(blocks):
                r, t = b // 2, b % 2
                partial = jnp.dot(block, out_weight, preferred_element_type=jnp.float32).astype(
                    jnp.bfloat16
                )
                if b:
                    pairs = [(h * 2 + l, (h ^ r) * 2 + (l ^ t)) for h in range(4) for l in range(2)]
                    partial = lax.ppermute(partial, SEQ, pairs)
                source = (chip ^ r) * 2 + (core ^ t)
                by_row = lax.dynamic_update_slice(
                    by_row, partial[None], (source // 2, 0, (source % 2) * width)
                )
            ordered = lax.psum_scatter(by_row, "chan", scatter_dimension=0, tiled=True)[0]
            return (residual.astype(jnp.float32) + ordered.astype(jnp.float32)).astype(jnp.bfloat16)
        gathered = gather_seq(local_context)
        group = seq_count // chan_count
        chunks = 2
        width = out_weight.shape[1] // chunks
        reduced = []
        for j in range(chunks):
            partial = jnp.dot(
                gathered, out_weight[:, j * width : (j + 1) * width], preferred_element_type=jnp.float32
            ).astype(jnp.bfloat16)
            by_row = lax.all_to_all(partial, SEQ, split_axis=0, concat_axis=1, tiled=True)
            reduced.append(
                lax.psum_scatter(by_row, "chan", scatter_dimension=1, tiled=True)
            )
        ordered = jnp.concatenate(
            [part[:, b * width : (b + 1) * width] for b in range(group) for part in reduced], axis=1
        )
        return (residual.astype(jnp.float32) + ordered.astype(jnp.float32)).astype(jnp.bfloat16)

    return per_device


def solution(mesh):
    seq_size, chan_size = mesh.devices.shape
    n_lo = cores_per_chip_along_seq(mesh)
    split = Mesh(
        mesh.devices.reshape(seq_size // n_lo, n_lo, chan_size), ("hi", "lo", mesh.axis_names[1])
    )
    rows_cols = P(SEQ, "chan")
    placed = (rows_cols, rows_cols, rows_cols, rows_cols, P("chan", SEQ))
    return jax.shard_map(
        make_per_device(is_square_of_chips(mesh, n_lo)),
        mesh=split,
        in_specs=placed,
        out_specs=rows_cols,
        check_vma=False,
    )
```

```python
import math

import jax
import jax.numpy as jnp
import numpy as np
from jax import lax
from jax.sharding import Mesh
from jax.sharding import PartitionSpec as P

HEAD_DIM = 128
SEQ = ("hi", "lo")


def cores_per_chip_along_seq(mesh):
    column = mesh.devices[:, 0]
    first = tuple(column[0].coords)
    count = 1
    while count < len(column) and tuple(column[count].coords) == first:
        count += 1
    return count


def is_square_of_chips(mesh, n_lo):
    column = mesh.devices[::n_lo, 0]
    if n_lo != 2 or len(column) != 4:
        return False
    coords = [np.array(d.coords) for d in column]
    for i in range(4):
        for flip in (1, 2):
            if np.abs(coords[i] - coords[i ^ flip]).sum() != 1:
                return False
    return True


def swap(axis, flip, n):
    return [(i, i ^ flip) for i in range(n)]


def assemble(pieces, rows, width, dtype):
    out = jnp.zeros((len(pieces) * rows, width), dtype)
    for piece, slot in pieces:
        out = lax.dynamic_update_slice(out, piece, (slot * rows, 0))
    return out


def gather_seq_square(x):
    rows, width = x.shape
    half = rows // 2
    chip = lax.axis_index("hi")
    core = lax.axis_index("lo")
    from_x = lax.ppermute(x, "hi", swap("hi", 1, 4))
    from_y = lax.ppermute(x, "hi", swap("hi", 2, 4))
    diag = jnp.concatenate(
        [
            lax.ppermute(from_y[:half], "hi", swap("hi", 1, 4)),
            lax.ppermute(from_x[half:], "hi", swap("hi", 2, 4)),
        ],
        axis=0,
    )
    mine = [(x, chip), (from_x, chip ^ 1), (from_y, chip ^ 2), (diag, chip ^ 3)]
    pieces = []
    for block, source in mine:
        pieces.append((block, source * 2 + core))
        pieces.append((lax.ppermute(block, "lo", [(0, 1), (1, 0)]), source * 2 + (1 - core)))
    return assemble(pieces, rows, width, x.dtype)


def gather_blocks_square(x):
    half = x.shape[0] // 2
    from_x = lax.ppermute(x, "hi", swap("hi", 1, 4))
    from_y = lax.ppermute(x, "hi", swap("hi", 2, 4))
    diag = jnp.concatenate(
        [
            lax.ppermute(from_y[:half], "hi", swap("hi", 1, 4)),
            lax.ppermute(from_x[half:], "hi", swap("hi", 2, 4)),
        ],
        axis=0,
    )
    blocks = []
    for block in (x, from_x, from_y, diag):
        blocks.append(block)
        blocks.append(lax.ppermute(block, "lo", [(0, 1), (1, 0)]))
    return blocks


def attention_by_head(queries, key_blocks, value_blocks, row_pos, key_starts):
    score_scale = 1.0 / math.sqrt(HEAD_DIM)
    scores = []
    masks = []
    for keys, start in zip(key_blocks, key_starts):
        part = (
            jnp.einsum("hqd,hkd->hqk", queries, keys, preferred_element_type=jnp.float32)
            * score_scale
        )
        key_pos = start + jnp.arange(keys.shape[1], dtype=jnp.int32)
        allowed = (key_pos[None, :] <= row_pos[:, None])[None]
        scores.append(jnp.where(allowed, part, -1e30))
        masks.append(allowed)
    row_max = scores[0].max(axis=-1)
    for part in scores[1:]:
        row_max = jnp.maximum(row_max, part.max(axis=-1))
    row_total = None
    numer = None
    for part, allowed, values in zip(scores, masks, value_blocks):
        weights = jnp.where(allowed, jnp.exp(part - row_max[..., None]), 0.0)
        total = jnp.sum(weights, axis=-1)
        term = jnp.einsum(
            "hqk,hkd->hqd", weights.astype(jnp.bfloat16), values, preferred_element_type=jnp.float32
        )
        row_total = total if row_total is None else row_total + total
        numer = term if numer is None else numer + term
    return numer / row_total[..., None]


def make_per_device(square):
    def gather_seq(x):
        if square:
            return gather_seq_square(x)
        return lax.all_gather(x, SEQ, axis=0, tiled=True)

    def per_device(query_proj, key_proj, value_proj, residual, out_weight):
        seg_rows = query_proj.shape[0]
        feat_width = query_proj.shape[1]
        heads_here = feat_width // HEAD_DIM
        seq_count = lax.axis_size("hi") * lax.axis_size("lo")
        chan_count = lax.axis_size("chan")
        segment = lax.axis_index("hi") * lax.axis_size("lo") + lax.axis_index("lo")
        score_scale = 1.0 / math.sqrt(HEAD_DIM)

        row_pos = segment * seg_rows + jnp.arange(seg_rows, dtype=jnp.int32)
        if square:
            def by_head(x):
                return x.reshape(seg_rows, heads_here, HEAD_DIM).transpose(1, 0, 2)

            key_blocks = gather_blocks_square(by_head(key_proj))
            value_blocks = gather_blocks_square(by_head(value_proj))
            chip = lax.axis_index("hi")
            core = lax.axis_index("lo")
            key_starts = [
                ((chip ^ (b // 2)) * 2 + (core ^ (b % 2))) * seg_rows for b in range(len(key_blocks))
            ]
            query_after, _ = lax.optimization_barrier((query_proj, key_blocks[2]))
            ratio = attention_by_head(by_head(query_after), key_blocks, value_blocks, row_pos, key_starts)
        else:
            both = gather_seq(jnp.concatenate([key_proj, value_proj], axis=1))
            total_rows = both.shape[0]
            keys = both[:, :feat_width].reshape(total_rows, heads_here, HEAD_DIM)
            values = both[:, feat_width:].reshape(total_rows, heads_here, HEAD_DIM)
            key_pos = jnp.arange(total_rows, dtype=jnp.int32)
            queries = query_proj.reshape(seg_rows, heads_here, HEAD_DIM)
            scores = (
                jnp.einsum("qhd,khd->hqk", queries, keys, preferred_element_type=jnp.float32)
                * score_scale
            )
            allowed = (key_pos[None, :] <= row_pos[:, None])[None]
            scores = jnp.where(allowed, scores, -1e30)
            row_max = jnp.max(scores, axis=-1)
            weights = jnp.where(allowed, jnp.exp(scores - row_max[..., None]), 0.0)
            row_total = jnp.sum(weights, axis=-1)
            numer = jnp.einsum(
                "hqk,khd->hqd", weights.astype(jnp.bfloat16), values, preferred_element_type=jnp.float32
            )
            ratio = numer / row_total[..., None]
        local_context = ratio.transpose(1, 0, 2).reshape(seg_rows, feat_width).astype(jnp.bfloat16)

        if square:
            chip = lax.axis_index("hi")
            core = lax.axis_index("lo")
            blocks = gather_blocks_square(local_context)
            width = out_weight.shape[1]
            by_row = jnp.zeros((chan_count, seg_rows, 2 * width), jnp.bfloat16)
            own_partial = jnp.dot(blocks[0], out_weight, preferred_element_type=jnp.float32).astype(
                jnp.bfloat16
            )
            own_partial, blocks[2] = lax.optimization_barrier((own_partial, blocks[2]))
            for b, block in enumerate(blocks):
                r, t = b // 2, b % 2
                if b == 0:
                    partial = own_partial
                else:
                    partial = jnp.dot(block, out_weight, preferred_element_type=jnp.float32).astype(
                        jnp.bfloat16
                    )
                if b:
                    pairs = [(h * 2 + l, (h ^ r) * 2 + (l ^ t)) for h in range(4) for l in range(2)]
                    partial = lax.ppermute(partial, SEQ, pairs)
                source = (chip ^ r) * 2 + (core ^ t)
                by_row = lax.dynamic_update_slice(
                    by_row, partial[None], (source // 2, 0, (source % 2) * width)
                )
            ordered = lax.psum_scatter(by_row, "chan", scatter_dimension=0, tiled=True)[0]
            return (residual.astype(jnp.float32) + ordered.astype(jnp.float32)).astype(jnp.bfloat16)
        gathered = gather_seq(local_context)
        group = seq_count // chan_count
        chunks = 2
        width = out_weight.shape[1] // chunks
        reduced = []
        for j in range(chunks):
            partial = jnp.dot(
                gathered, out_weight[:, j * width : (j + 1) * width], preferred_element_type=jnp.float32
            ).astype(jnp.bfloat16)
            by_row = lax.all_to_all(partial, SEQ, split_axis=0, concat_axis=1, tiled=True)
            reduced.append(
                lax.psum_scatter(by_row, "chan", scatter_dimension=1, tiled=True)
            )
        ordered = jnp.concatenate(
            [part[:, b * width : (b + 1) * width] for b in range(group) for part in reduced], axis=1
        )
        return (residual.astype(jnp.float32) + ordered.astype(jnp.float32)).astype(jnp.bfloat16)

    return per_device


def solution(mesh):
    seq_size, chan_size = mesh.devices.shape
    n_lo = cores_per_chip_along_seq(mesh)
    split = Mesh(
        mesh.devices.reshape(seq_size // n_lo, n_lo, chan_size), ("hi", "lo", mesh.axis_names[1])
    )
    rows_cols = P(SEQ, "chan")
    placed = (rows_cols, rows_cols, rows_cols, rows_cols, P("chan", SEQ))
    return jax.shard_map(
        make_per_device(is_square_of_chips(mesh, n_lo)),
        mesh=split,
        in_specs=placed,
        out_specs=rows_cols,
        check_vma=False,
    )
```

```python
import math

import jax
import jax.numpy as jnp
import numpy as np
from jax import lax
from jax.sharding import Mesh
from jax.sharding import PartitionSpec as P

HEAD_DIM = 128
SEQ = ("hi", "lo")


def cores_per_chip_along_seq(mesh):
    column = mesh.devices[:, 0]
    first = tuple(column[0].coords)
    count = 1
    while count < len(column) and tuple(column[count].coords) == first:
        count += 1
    return count


def is_square_of_chips(mesh, n_lo):
    column = mesh.devices[::n_lo, 0]
    if n_lo != 2 or len(column) != 4:
        return False
    coords = [np.array(d.coords) for d in column]
    for i in range(4):
        for flip in (1, 2):
            if np.abs(coords[i] - coords[i ^ flip]).sum() != 1:
                return False
    return True


def swap(axis, flip, n):
    return [(i, i ^ flip) for i in range(n)]


def assemble(pieces, rows, width, dtype):
    out = jnp.zeros((len(pieces) * rows, width), dtype)
    for piece, slot in pieces:
        out = lax.dynamic_update_slice(out, piece, (slot * rows, 0))
    return out


def gather_seq_square(x):
    rows, width = x.shape
    half = rows // 2
    chip = lax.axis_index("hi")
    core = lax.axis_index("lo")
    from_x = lax.ppermute(x, "hi", swap("hi", 1, 4))
    from_y = lax.ppermute(x, "hi", swap("hi", 2, 4))
    diag = jnp.concatenate(
        [
            lax.ppermute(from_y[:half], "hi", swap("hi", 1, 4)),
            lax.ppermute(from_x[half:], "hi", swap("hi", 2, 4)),
        ],
        axis=0,
    )
    mine = [(x, chip), (from_x, chip ^ 1), (from_y, chip ^ 2), (diag, chip ^ 3)]
    pieces = []
    for block, source in mine:
        pieces.append((block, source * 2 + core))
        pieces.append((lax.ppermute(block, "lo", [(0, 1), (1, 0)]), source * 2 + (1 - core)))
    return assemble(pieces, rows, width, x.dtype)


def gather_blocks_square(x):
    half = x.shape[0] // 2
    from_x = lax.ppermute(x, "hi", swap("hi", 1, 4))
    from_y = lax.ppermute(x, "hi", swap("hi", 2, 4))
    diag = jnp.concatenate(
        [
            lax.ppermute(from_y[:half], "hi", swap("hi", 1, 4)),
            lax.ppermute(from_x[half:], "hi", swap("hi", 2, 4)),
        ],
        axis=0,
    )
    blocks = []
    for block in (x, from_x, from_y, diag):
        blocks.append(block)
        blocks.append(lax.ppermute(block, "lo", [(0, 1), (1, 0)]))
    return blocks


def attention_by_head(queries, key_blocks, value_blocks, row_pos, key_starts):
    score_scale = 1.0 / math.sqrt(HEAD_DIM)
    scores = []
    masks = []
    for keys, start in zip(key_blocks, key_starts):
        part = (
            jnp.einsum("hqd,hkd->hqk", queries, keys, preferred_element_type=jnp.float32)
            * score_scale
        )
        key_pos = start + jnp.arange(keys.shape[1], dtype=jnp.int32)
        allowed = (key_pos[None, :] <= row_pos[:, None])[None]
        scores.append(jnp.where(allowed, part, -1e30))
        masks.append(allowed)
    row_max = scores[0].max(axis=-1)
    for part in scores[1:]:
        row_max = jnp.maximum(row_max, part.max(axis=-1))
    row_total = None
    numer = None
    for part, allowed, values in zip(scores, masks, value_blocks):
        weights = jnp.where(allowed, jnp.exp(part - row_max[..., None]), 0.0)
        total = jnp.sum(weights, axis=-1)
        term = jnp.einsum(
            "hqk,hkd->hqd", weights.astype(jnp.bfloat16), values, preferred_element_type=jnp.float32
        )
        row_total = total if row_total is None else row_total + total
        numer = term if numer is None else numer + term
    return numer / row_total[..., None]


def make_per_device(square):
    def gather_seq(x):
        if square:
            return gather_seq_square(x)
        return lax.all_gather(x, SEQ, axis=0, tiled=True)

    def per_device(query_proj, key_proj, value_proj, residual, out_weight):
        seg_rows = query_proj.shape[0]
        feat_width = query_proj.shape[1]
        heads_here = feat_width // HEAD_DIM
        seq_count = lax.axis_size("hi") * lax.axis_size("lo")
        chan_count = lax.axis_size("chan")
        segment = lax.axis_index("hi") * lax.axis_size("lo") + lax.axis_index("lo")
        score_scale = 1.0 / math.sqrt(HEAD_DIM)

        row_pos = segment * seg_rows + jnp.arange(seg_rows, dtype=jnp.int32)
        if square:
            def by_head(x):
                return x.reshape(seg_rows, heads_here, HEAD_DIM).transpose(1, 0, 2)

            key_blocks = gather_blocks_square(by_head(key_proj))
            value_blocks = gather_blocks_square(by_head(value_proj))
            chip = lax.axis_index("hi")
            core = lax.axis_index("lo")
            key_starts = [
                ((chip ^ (b // 2)) * 2 + (core ^ (b % 2))) * seg_rows for b in range(len(key_blocks))
            ]
            query_after, _ = lax.optimization_barrier((query_proj, key_blocks[2]))
            ratio = attention_by_head(by_head(query_after), key_blocks, value_blocks, row_pos, key_starts)
        else:
            both = gather_seq(jnp.concatenate([key_proj, value_proj], axis=1))
            total_rows = both.shape[0]
            keys = both[:, :feat_width].reshape(total_rows, heads_here, HEAD_DIM)
            values = both[:, feat_width:].reshape(total_rows, heads_here, HEAD_DIM)
            key_pos = jnp.arange(total_rows, dtype=jnp.int32)
            queries = query_proj.reshape(seg_rows, heads_here, HEAD_DIM)
            scores = (
                jnp.einsum("qhd,khd->hqk", queries, keys, preferred_element_type=jnp.float32)
                * score_scale
            )
            allowed = (key_pos[None, :] <= row_pos[:, None])[None]
            scores = jnp.where(allowed, scores, -1e30)
            row_max = jnp.max(scores, axis=-1)
            weights = jnp.where(allowed, jnp.exp(scores - row_max[..., None]), 0.0)
            row_total = jnp.sum(weights, axis=-1)
            numer = jnp.einsum(
                "hqk,khd->hqd", weights.astype(jnp.bfloat16), values, preferred_element_type=jnp.float32
            )
            ratio = numer / row_total[..., None]
        local_context = ratio.transpose(1, 0, 2).reshape(seg_rows, feat_width).astype(jnp.bfloat16)

        if square:
            chip = lax.axis_index("hi")
            core = lax.axis_index("lo")
            blocks = gather_blocks_square(local_context)
            width = out_weight.shape[1]
            chan_index = lax.axis_index("chan")
            by_row = jnp.zeros((chan_count, seg_rows, 2 * width), jnp.bfloat16)
            own_partial = jnp.dot(blocks[0], out_weight, preferred_element_type=jnp.float32).astype(
                jnp.bfloat16
            )
            own_partial, blocks[2] = lax.optimization_barrier((own_partial, blocks[2]))
            for b, block in enumerate(blocks):
                r, t = b // 2, b % 2
                if b == 0:
                    partial = own_partial
                else:
                    partial = jnp.dot(block, out_weight, preferred_element_type=jnp.float32).astype(
                        jnp.bfloat16
                    )
                if b:
                    pairs = [(h * 2 + l, (h ^ r) * 2 + (l ^ t)) for h in range(4) for l in range(2)]
                    partial = lax.ppermute(partial, SEQ, pairs)
                source = (chip ^ r) * 2 + (core ^ t)
                residual_part = lax.dynamic_slice_in_dim(residual, (source % 2) * width, width, 1)
                partial = jnp.where(
                    source // 2 == chan_index,
                    (partial.astype(jnp.float32) + residual_part.astype(jnp.float32)).astype(
                        jnp.bfloat16
                    ),
                    partial,
                )
                by_row = lax.dynamic_update_slice(
                    by_row, partial[None], (source // 2, 0, (source % 2) * width)
                )
            return lax.psum_scatter(by_row, "chan", scatter_dimension=0, tiled=True)[0]
        gathered = gather_seq(local_context)
        group = seq_count // chan_count
        chunks = 2
        width = out_weight.shape[1] // chunks
        reduced = []
        for j in range(chunks):
            partial = jnp.dot(
                gathered, out_weight[:, j * width : (j + 1) * width], preferred_element_type=jnp.float32
            ).astype(jnp.bfloat16)
            by_row = lax.all_to_all(partial, SEQ, split_axis=0, concat_axis=1, tiled=True)
            reduced.append(
                lax.psum_scatter(by_row, "chan", scatter_dimension=1, tiled=True)
            )
        ordered = jnp.concatenate(
            [part[:, b * width : (b + 1) * width] for b in range(group) for part in reduced], axis=1
        )
        return (residual.astype(jnp.float32) + ordered.astype(jnp.float32)).astype(jnp.bfloat16)

    return per_device


def solution(mesh):
    seq_size, chan_size = mesh.devices.shape
    n_lo = cores_per_chip_along_seq(mesh)
    split = Mesh(
        mesh.devices.reshape(seq_size // n_lo, n_lo, chan_size), ("hi", "lo", mesh.axis_names[1])
    )
    rows_cols = P(SEQ, "chan")
    placed = (rows_cols, rows_cols, rows_cols, rows_cols, P("chan", SEQ))
    return jax.shard_map(
        make_per_device(is_square_of_chips(mesh, n_lo)),
        mesh=split,
        in_specs=placed,
        out_specs=rows_cols,
        check_vma=False,
    )
```

```python
import math

import jax
import jax.numpy as jnp
import numpy as np
from jax import lax
from jax.sharding import Mesh
from jax.sharding import PartitionSpec as P

HEAD_DIM = 128
SEQ = ("hi", "lo")


def cores_per_chip_along_seq(mesh):
    column = mesh.devices[:, 0]
    first = tuple(column[0].coords)
    count = 1
    while count < len(column) and tuple(column[count].coords) == first:
        count += 1
    return count


def is_square_of_chips(mesh, n_lo):
    column = mesh.devices[::n_lo, 0]
    if n_lo != 2 or len(column) != 4:
        return False
    coords = [np.array(d.coords) for d in column]
    for i in range(4):
        for flip in (1, 2):
            if np.abs(coords[i] - coords[i ^ flip]).sum() != 1:
                return False
    return True


def swap(axis, flip, n):
    return [(i, i ^ flip) for i in range(n)]


def assemble(pieces, rows, width, dtype):
    out = jnp.zeros((len(pieces) * rows, width), dtype)
    for piece, slot in pieces:
        out = lax.dynamic_update_slice(out, piece, (slot * rows, 0))
    return out


def gather_seq_square(x):
    rows, width = x.shape
    half = rows // 2
    chip = lax.axis_index("hi")
    core = lax.axis_index("lo")
    from_x = lax.ppermute(x, "hi", swap("hi", 1, 4))
    from_y = lax.ppermute(x, "hi", swap("hi", 2, 4))
    diag = jnp.concatenate(
        [
            lax.ppermute(from_y[:half], "hi", swap("hi", 1, 4)),
            lax.ppermute(from_x[half:], "hi", swap("hi", 2, 4)),
        ],
        axis=0,
    )
    mine = [(x, chip), (from_x, chip ^ 1), (from_y, chip ^ 2), (diag, chip ^ 3)]
    pieces = []
    for block, source in mine:
        pieces.append((block, source * 2 + core))
        pieces.append((lax.ppermute(block, "lo", [(0, 1), (1, 0)]), source * 2 + (1 - core)))
    return assemble(pieces, rows, width, x.dtype)


def gather_blocks_square(x):
    half = x.shape[0] // 2
    from_x = lax.ppermute(x, "hi", swap("hi", 1, 4))
    from_y = lax.ppermute(x, "hi", swap("hi", 2, 4))
    diag = jnp.concatenate(
        [
            lax.ppermute(from_y[:half], "hi", swap("hi", 1, 4)),
            lax.ppermute(from_x[half:], "hi", swap("hi", 2, 4)),
        ],
        axis=0,
    )
    blocks = []
    for block in (x, from_x, from_y, diag):
        blocks.append(block)
        blocks.append(lax.ppermute(block, "lo", [(0, 1), (1, 0)]))
    return blocks


def attention_by_head(queries, key_blocks, value_blocks, row_pos, key_starts):
    score_scale = 1.0 / math.sqrt(HEAD_DIM)
    scores = []
    masks = []
    for keys, start in zip(key_blocks, key_starts):
        part = (
            jnp.einsum("hqd,hkd->hqk", queries, keys, preferred_element_type=jnp.float32)
            * score_scale
        )
        key_pos = start + jnp.arange(keys.shape[1], dtype=jnp.int32)
        allowed = (key_pos[None, :] <= row_pos[:, None])[None]
        scores.append(jnp.where(allowed, part, -1e30))
        masks.append(allowed)
    row_max = scores[0].max(axis=-1)
    for part in scores[1:]:
        row_max = jnp.maximum(row_max, part.max(axis=-1))
    row_total = None
    numer = None
    for part, allowed, values in zip(scores, masks, value_blocks):
        weights = jnp.where(allowed, jnp.exp(part - row_max[..., None]), 0.0)
        total = jnp.sum(weights, axis=-1)
        term = jnp.einsum(
            "hqk,hkd->hqd", weights.astype(jnp.bfloat16), values, preferred_element_type=jnp.float32
        )
        row_total = total if row_total is None else row_total + total
        numer = term if numer is None else numer + term
    return numer / row_total[..., None]


def make_per_device(square):
    def gather_seq(x):
        if square:
            return gather_seq_square(x)
        return lax.all_gather(x, SEQ, axis=0, tiled=True)

    def per_device(query_proj, key_proj, value_proj, residual, out_weight):
        seg_rows = query_proj.shape[0]
        feat_width = query_proj.shape[1]
        heads_here = feat_width // HEAD_DIM
        seq_count = lax.axis_size("hi") * lax.axis_size("lo")
        chan_count = lax.axis_size("chan")
        segment = lax.axis_index("hi") * lax.axis_size("lo") + lax.axis_index("lo")
        score_scale = 1.0 / math.sqrt(HEAD_DIM)

        row_pos = segment * seg_rows + jnp.arange(seg_rows, dtype=jnp.int32)
        if square:
            def by_head(x):
                return x.reshape(seg_rows, heads_here, HEAD_DIM).transpose(1, 0, 2)

            key_blocks = gather_blocks_square(by_head(key_proj))
            value_blocks = gather_blocks_square(by_head(value_proj))
            chip = lax.axis_index("hi")
            core = lax.axis_index("lo")
            key_starts = [
                ((chip ^ (b // 2)) * 2 + (core ^ (b % 2))) * seg_rows for b in range(len(key_blocks))
            ]
            query_after, _ = lax.optimization_barrier((query_proj, key_blocks[2]))
            ratio = attention_by_head(by_head(query_after), key_blocks, value_blocks, row_pos, key_starts)
        else:
            both = gather_seq(jnp.concatenate([key_proj, value_proj], axis=1))
            total_rows = both.shape[0]
            keys = both[:, :feat_width].reshape(total_rows, heads_here, HEAD_DIM)
            values = both[:, feat_width:].reshape(total_rows, heads_here, HEAD_DIM)
            key_pos = jnp.arange(total_rows, dtype=jnp.int32)
            queries = query_proj.reshape(seg_rows, heads_here, HEAD_DIM)
            scores = (
                jnp.einsum("qhd,khd->hqk", queries, keys, preferred_element_type=jnp.float32)
                * score_scale
            )
            allowed = (key_pos[None, :] <= row_pos[:, None])[None]
            scores = jnp.where(allowed, scores, -1e30)
            row_max = jnp.max(scores, axis=-1)
            weights = jnp.where(allowed, jnp.exp(scores - row_max[..., None]), 0.0)
            row_total = jnp.sum(weights, axis=-1)
            numer = jnp.einsum(
                "hqk,khd->hqd", weights.astype(jnp.bfloat16), values, preferred_element_type=jnp.float32
            )
            ratio = numer / row_total[..., None]
        local_context = ratio.transpose(1, 0, 2).reshape(seg_rows, feat_width).astype(jnp.bfloat16)

        if square:
            chip = lax.axis_index("hi")
            core = lax.axis_index("lo")
            blocks = gather_blocks_square(local_context)
            width = out_weight.shape[1]
            chan_index = lax.axis_index("chan")
            by_row = jnp.zeros((chan_count, seg_rows, 2 * width), jnp.bfloat16)
            own_partial = jnp.dot(blocks[0], out_weight, preferred_element_type=jnp.float32).astype(
                jnp.bfloat16
            )
            own_partial, blocks[2] = lax.optimization_barrier((own_partial, blocks[2]))
            diagonal = jnp.dot(
                jnp.concatenate(blocks[6:], axis=0), out_weight, preferred_element_type=jnp.float32
            ).astype(jnp.bfloat16)
            for b, block in enumerate(blocks):
                r, t = b // 2, b % 2
                if b == 0:
                    partial = own_partial
                elif b >= 6:
                    partial = diagonal[(b - 6) * seg_rows : (b - 5) * seg_rows]
                else:
                    partial = jnp.dot(block, out_weight, preferred_element_type=jnp.float32).astype(
                        jnp.bfloat16
                    )
                if b:
                    pairs = [(h * 2 + l, (h ^ r) * 2 + (l ^ t)) for h in range(4) for l in range(2)]
                    partial = lax.ppermute(partial, SEQ, pairs)
                source = (chip ^ r) * 2 + (core ^ t)
                residual_part = lax.dynamic_slice_in_dim(residual, (source % 2) * width, width, 1)
                partial = jnp.where(
                    source // 2 == chan_index,
                    (partial.astype(jnp.float32) + residual_part.astype(jnp.float32)).astype(
                        jnp.bfloat16
                    ),
                    partial,
                )
                by_row = lax.dynamic_update_slice(
                    by_row, partial[None], (source // 2, 0, (source % 2) * width)
                )
            return lax.psum_scatter(by_row, "chan", scatter_dimension=0, tiled=True)[0]
        gathered = gather_seq(local_context)
        group = seq_count // chan_count
        chunks = 2
        width = out_weight.shape[1] // chunks
        reduced = []
        for j in range(chunks):
            partial = jnp.dot(
                gathered, out_weight[:, j * width : (j + 1) * width], preferred_element_type=jnp.float32
            ).astype(jnp.bfloat16)
            by_row = lax.all_to_all(partial, SEQ, split_axis=0, concat_axis=1, tiled=True)
            reduced.append(
                lax.psum_scatter(by_row, "chan", scatter_dimension=1, tiled=True)
            )
        ordered = jnp.concatenate(
            [part[:, b * width : (b + 1) * width] for b in range(group) for part in reduced], axis=1
        )
        return (residual.astype(jnp.float32) + ordered.astype(jnp.float32)).astype(jnp.bfloat16)

    return per_device


def solution(mesh):
    seq_size, chan_size = mesh.devices.shape
    n_lo = cores_per_chip_along_seq(mesh)
    split = Mesh(
        mesh.devices.reshape(seq_size // n_lo, n_lo, chan_size), ("hi", "lo", mesh.axis_names[1])
    )
    rows_cols = P(SEQ, "chan")
    placed = (rows_cols, rows_cols, rows_cols, rows_cols, P("chan", SEQ))
    return jax.shard_map(
        make_per_device(is_square_of_chips(mesh, n_lo)),
        mesh=split,
        in_specs=placed,
        out_specs=rows_cols,
        check_vma=False,
    )
```

```python
import math

import jax
import jax.numpy as jnp
import numpy as np
from jax import lax
from jax.sharding import Mesh
from jax.sharding import PartitionSpec as P

HEAD_DIM = 128
SEQ = ("hi", "lo")


def cores_per_chip_along_seq(mesh):
    column = mesh.devices[:, 0]
    first = tuple(column[0].coords)
    count = 1
    while count < len(column) and tuple(column[count].coords) == first:
        count += 1
    return count


def is_square_of_chips(mesh, n_lo):
    column = mesh.devices[::n_lo, 0]
    if n_lo != 2 or len(column) != 4:
        return False
    coords = [np.array(d.coords) for d in column]
    for i in range(4):
        for flip in (1, 2):
            if np.abs(coords[i] - coords[i ^ flip]).sum() != 1:
                return False
    return True


def swap(axis, flip, n):
    return [(i, i ^ flip) for i in range(n)]


def assemble(pieces, rows, width, dtype):
    out = jnp.zeros((len(pieces) * rows, width), dtype)
    for piece, slot in pieces:
        out = lax.dynamic_update_slice(out, piece, (slot * rows, 0))
    return out


def gather_seq_square(x):
    rows, width = x.shape
    half = rows // 2
    chip = lax.axis_index("hi")
    core = lax.axis_index("lo")
    from_x = lax.ppermute(x, "hi", swap("hi", 1, 4))
    from_y = lax.ppermute(x, "hi", swap("hi", 2, 4))
    diag = jnp.concatenate(
        [
            lax.ppermute(from_y[:half], "hi", swap("hi", 1, 4)),
            lax.ppermute(from_x[half:], "hi", swap("hi", 2, 4)),
        ],
        axis=0,
    )
    mine = [(x, chip), (from_x, chip ^ 1), (from_y, chip ^ 2), (diag, chip ^ 3)]
    pieces = []
    for block, source in mine:
        pieces.append((block, source * 2 + core))
        pieces.append((lax.ppermute(block, "lo", [(0, 1), (1, 0)]), source * 2 + (1 - core)))
    return assemble(pieces, rows, width, x.dtype)


def gather_blocks_square(x):
    half = x.shape[0] // 2
    from_x = lax.ppermute(x, "hi", swap("hi", 1, 4))
    from_y = lax.ppermute(x, "hi", swap("hi", 2, 4))
    diag = jnp.concatenate(
        [
            lax.ppermute(from_y[:half], "hi", swap("hi", 1, 4)),
            lax.ppermute(from_x[half:], "hi", swap("hi", 2, 4)),
        ],
        axis=0,
    )
    blocks = []
    for block in (x, from_x, from_y, diag):
        blocks.append(block)
        blocks.append(lax.ppermute(block, "lo", [(0, 1), (1, 0)]))
    return blocks


def attention_by_head(queries, key_blocks, value_blocks, row_pos, key_starts):
    score_scale = 1.0 / math.sqrt(HEAD_DIM)
    scores = []
    masks = []
    raw = [
        jnp.einsum("hqd,hkd->hqk", queries, keys, preferred_element_type=jnp.float32)
        for keys in key_blocks[:2]
    ]
    raw[0], raw[1], _ = lax.optimization_barrier((raw[0], raw[1], key_blocks[2]))
    for i, (keys, start) in enumerate(zip(key_blocks, key_starts)):
        if i < 2:
            part = raw[i] * score_scale
        else:
            part = (
                jnp.einsum("hqd,hkd->hqk", queries, keys, preferred_element_type=jnp.float32)
                * score_scale
            )
        key_pos = start + jnp.arange(keys.shape[1], dtype=jnp.int32)
        allowed = (key_pos[None, :] <= row_pos[:, None])[None]
        scores.append(jnp.where(allowed, part, -1e30))
        masks.append(allowed)
    row_max = scores[0].max(axis=-1)
    for part in scores[1:]:
        row_max = jnp.maximum(row_max, part.max(axis=-1))
    row_total = None
    numer = None
    for part, allowed, values in zip(scores, masks, value_blocks):
        weights = jnp.where(allowed, jnp.exp(part - row_max[..., None]), 0.0)
        total = jnp.sum(weights, axis=-1)
        term = jnp.einsum(
            "hqk,hkd->hqd", weights.astype(jnp.bfloat16), values, preferred_element_type=jnp.float32
        )
        row_total = total if row_total is None else row_total + total
        numer = term if numer is None else numer + term
    return numer / row_total[..., None]


def make_per_device(square):
    def gather_seq(x):
        if square:
            return gather_seq_square(x)
        return lax.all_gather(x, SEQ, axis=0, tiled=True)

    def per_device(query_proj, key_proj, value_proj, residual, out_weight):
        seg_rows = query_proj.shape[0]
        feat_width = query_proj.shape[1]
        heads_here = feat_width // HEAD_DIM
        seq_count = lax.axis_size("hi") * lax.axis_size("lo")
        chan_count = lax.axis_size("chan")
        segment = lax.axis_index("hi") * lax.axis_size("lo") + lax.axis_index("lo")
        score_scale = 1.0 / math.sqrt(HEAD_DIM)

        row_pos = segment * seg_rows + jnp.arange(seg_rows, dtype=jnp.int32)
        if square:
            def by_head(x):
                return x.reshape(seg_rows, heads_here, HEAD_DIM).transpose(1, 0, 2)

            key_blocks = gather_blocks_square(by_head(key_proj))
            value_blocks = gather_blocks_square(by_head(value_proj))
            chip = lax.axis_index("hi")
            core = lax.axis_index("lo")
            key_starts = [
                ((chip ^ (b // 2)) * 2 + (core ^ (b % 2))) * seg_rows for b in range(len(key_blocks))
            ]
            query_after, _ = lax.optimization_barrier((query_proj, key_blocks[2]))
            ratio = attention_by_head(by_head(query_after), key_blocks, value_blocks, row_pos, key_starts)
        else:
            both = gather_seq(jnp.concatenate([key_proj, value_proj], axis=1))
            total_rows = both.shape[0]
            keys = both[:, :feat_width].reshape(total_rows, heads_here, HEAD_DIM)
            values = both[:, feat_width:].reshape(total_rows, heads_here, HEAD_DIM)
            key_pos = jnp.arange(total_rows, dtype=jnp.int32)
            queries = query_proj.reshape(seg_rows, heads_here, HEAD_DIM)
            scores = (
                jnp.einsum("qhd,khd->hqk", queries, keys, preferred_element_type=jnp.float32)
                * score_scale
            )
            allowed = (key_pos[None, :] <= row_pos[:, None])[None]
            scores = jnp.where(allowed, scores, -1e30)
            row_max = jnp.max(scores, axis=-1)
            weights = jnp.where(allowed, jnp.exp(scores - row_max[..., None]), 0.0)
            row_total = jnp.sum(weights, axis=-1)
            numer = jnp.einsum(
                "hqk,khd->hqd", weights.astype(jnp.bfloat16), values, preferred_element_type=jnp.float32
            )
            ratio = numer / row_total[..., None]
        local_context = ratio.transpose(1, 0, 2).reshape(seg_rows, feat_width).astype(jnp.bfloat16)

        if square:
            chip = lax.axis_index("hi")
            core = lax.axis_index("lo")
            blocks = gather_blocks_square(local_context)
            width = out_weight.shape[1]
            chan_index = lax.axis_index("chan")
            by_row = jnp.zeros((chan_count, seg_rows, 2 * width), jnp.bfloat16)
            own_partial = jnp.dot(blocks[0], out_weight, preferred_element_type=jnp.float32).astype(
                jnp.bfloat16
            )
            own_partial, blocks[2] = lax.optimization_barrier((own_partial, blocks[2]))
            for b, block in enumerate(blocks):
                r, t = b // 2, b % 2
                if b == 0:
                    partial = own_partial
                else:
                    partial = jnp.dot(block, out_weight, preferred_element_type=jnp.float32).astype(
                        jnp.bfloat16
                    )
                if b:
                    pairs = [(h * 2 + l, (h ^ r) * 2 + (l ^ t)) for h in range(4) for l in range(2)]
                    partial = lax.ppermute(partial, SEQ, pairs)
                source = (chip ^ r) * 2 + (core ^ t)
                residual_part = lax.dynamic_slice_in_dim(residual, (source % 2) * width, width, 1)
                partial = jnp.where(
                    source // 2 == chan_index,
                    (partial.astype(jnp.float32) + residual_part.astype(jnp.float32)).astype(
                        jnp.bfloat16
                    ),
                    partial,
                )
                by_row = lax.dynamic_update_slice(
                    by_row, partial[None], (source // 2, 0, (source % 2) * width)
                )
            return lax.psum_scatter(by_row, "chan", scatter_dimension=0, tiled=True)[0]
        gathered = gather_seq(local_context)
        group = seq_count // chan_count
        chunks = 2
        width = out_weight.shape[1] // chunks
        reduced = []
        for j in range(chunks):
            partial = jnp.dot(
                gathered, out_weight[:, j * width : (j + 1) * width], preferred_element_type=jnp.float32
            ).astype(jnp.bfloat16)
            by_row = lax.all_to_all(partial, SEQ, split_axis=0, concat_axis=1, tiled=True)
            reduced.append(
                lax.psum_scatter(by_row, "chan", scatter_dimension=1, tiled=True)
            )
        ordered = jnp.concatenate(
            [part[:, b * width : (b + 1) * width] for b in range(group) for part in reduced], axis=1
        )
        return (residual.astype(jnp.float32) + ordered.astype(jnp.float32)).astype(jnp.bfloat16)

    return per_device


def solution(mesh):
    seq_size, chan_size = mesh.devices.shape
    n_lo = cores_per_chip_along_seq(mesh)
    split = Mesh(
        mesh.devices.reshape(seq_size // n_lo, n_lo, chan_size), ("hi", "lo", mesh.axis_names[1])
    )
    rows_cols = P(SEQ, "chan")
    placed = (rows_cols, rows_cols, rows_cols, rows_cols, P("chan", SEQ))
    return jax.shard_map(
        make_per_device(is_square_of_chips(mesh, n_lo)),
        mesh=split,
        in_specs=placed,
        out_specs=rows_cols,
        check_vma=False,
    )
```
